512 devices in a mesh: cells: 128 (over x, z_hi, y), modes: 4 (over z_lo, core).
Axes of the slice: x: 4, y: 8, z: 8 (z_hi: 4, z_lo: 2; z = z_hi * 2 + z_lo), core: 2. Of those that a mesh axis runs over, the one named last changes fastest.
Arguments:
- fields: bfloat16 [84, 4, 2048, 128], P('modes', None, 'cells'), may hold values from -1.5 to 1.5
- coupling: bfloat16 [7, 84, 84], replicated, may hold values from -0.625 to 0.625
- kl_field: float32 [7, 2048, 128], P(None, 'cells'), may hold values from -5 to 5
- material: int32 [2048, 128], P('cells'), may hold values from 0 to 7
- char_state: int32 [2048, 128], P('cells'), may hold values from 0 to 2
- material_table: float32 [7, 8], replicated, may hold values from 0.5 to 2
- char_table: float32 [7, 3], replicated, may hold values from 0.3 to 1.5
- expansion_table: float32 [7, 8], replicated, may hold values from 1 to 4
Outputs:
- response: bfloat16 [84, 4, 2048, 128], P('modes', None, 'cells')
The draws below stay inside these ranges and needn't reach their ends.
All inputs are finite; a program needn't handle non-finite values.
Results may differ from the reference program's by a relative error of at most 0.0049.
Values may be sent and summed in bfloat16 or wider, within the bound.
No kernel may reach another device: no remote copies, remote signals or barrier semaphores. Data moves between devices by JAX's collectives and lax.ppermute only.
A program may use at most 64 MiB of HBM per device.

```python
import math
import jax
import jax.numpy as jnp
from jax import lax

P_SIZE = 84
F = 4
K = 7
M = 8
Q = 3
NY = 128
NX = 2048


def set_ends(array, rng, smallest, top_value):
    longest = array.shape.index(max(array.shape))
    spots = []
    for shift in (0, 1):
        where = [jax.random.randint(jax.random.fold_in(rng, axis), (), 0, length) for axis, length in enumerate(array.shape)]
        where[longest] = (where[longest] + shift) % array.shape[longest]
        spots.append(tuple(where))
    return array.at[spots[0]].set(smallest).at[spots[1]].set(top_value)


def block_scale(key, shape, shards, low, high):
    factor_of = 1.0
    for position, parts in shards:
        heights = jax.random.uniform(jax.random.fold_in(jax.random.fold_in(key, 6), position), (parts,), jnp.float32, low / len(shards), high / len(shards))
        factor_of = factor_of * jnp.repeat(jnp.exp(heights), shape[position] // parts).reshape((-1,) + (1,) * (len(shape) - 1 - position))
    return factor_of


def scatter_about(rng, dims, deviation, limit, pieces=(), kind=jnp.bfloat16):
    array = deviation * jax.random.normal(rng, dims, jnp.float32)
    if pieces:
        array = array * block_scale(rng, dims, pieces, -0.22, 0.18)
    return jnp.clip(array, -limit, limit).astype(kind)


def setup_inputs(seed: int = 0) -> dict:
    splits = jax.random.split(jax.random.key(seed), 9)
    fields = scatter_about(splits[0], (P_SIZE, F, NX, NY), 0.25, 1.5, ((0, 4), (2, 128)))
    coupling = scatter_about(splits[1], (K, P_SIZE, P_SIZE), P_SIZE ** -0.5, 0.625)
    kl_field = scatter_about(splits[2], (K, NX, NY), 1.0, 5.0, ((1, 128),), jnp.float32)
    material = set_ends(jax.random.randint(splits[3], (NX, NY), 0, M), jax.random.fold_in(splits[3], 1), 0, M - 1).astype(jnp.int32)
    char_state = set_ends(jax.random.randint(splits[4], (NX, NY), 0, Q), jax.random.fold_in(splits[4], 1), 0, Q - 1).astype(jnp.int32)
    material_table = jnp.clip(jnp.exp(jax.random.uniform(splits[5], (K, M), jnp.float32, math.log(0.5), math.log(2.0))), 0.5, 2.0)
    char_table = jnp.clip(jnp.exp(jax.random.uniform(splits[6], (K, Q), jnp.float32, math.log(0.3), math.log(1.5))), 0.3, 1.5)
    expansion_table = jnp.clip(jnp.exp(jax.random.uniform(splits[7], (K, M), jnp.float32, math.log(1.0), math.log(4.0))), 1.0, 4.0)
    return dict(fields=fields, coupling=coupling, kl_field=kl_field, material=material, char_state=char_state, material_table=material_table, char_table=char_table, expansion_table=expansion_table)


def derive(rimmed):
    center = rimmed[:, :, 1:-1].astype(jnp.float32)
    above_row = rimmed[:, :, :-2].astype(jnp.float32)
    below_row = rimmed[:, :, 2:].astype(jnp.float32)
    zero_col = jnp.zeros(center.shape[:3] + (1,), jnp.float32)
    left_col = jnp.concatenate([zero_col, center[..., :-1]], axis=3)
    right_col = jnp.concatenate([center[..., 1:], zero_col], axis=3)
    laplace = 4.0 * center - above_row - below_row - left_col - right_col
    grad_x = 0.5 * (below_row[:, 0:1] - above_row[:, 0:1])
    grad_y = 0.5 * (right_col[:, 0:1] - left_col[:, 0:1])
    return jnp.concatenate([laplace, grad_x, grad_y], axis=1).astype(jnp.bfloat16)


def reference(fields, coupling, kl_field, material, char_state, material_table, char_table, expansion_table):
    cond = kl_field * material_table[:, material] * char_table[:, char_state]
    expand = kl_field * expansion_table[:, material]
    weights = coupling.astype(jnp.float32)
    nfield = fields.shape[1]
    height = math.gcd(NX, 4)

    def advance(block_index, result):
        first_row = (block_index * height).astype(jnp.int32)
        middle = lax.dynamic_slice_in_dim(fields, first_row, height, 2)
        above_idx = jnp.maximum(first_row - 1, 0).astype(jnp.int32)
        below_idx = jnp.minimum(first_row + height, NX - 1).astype(jnp.int32)
        above_row = lax.dynamic_slice_in_dim(fields, above_idx, 1, 2)
        below_row = lax.dynamic_slice_in_dim(fields, below_idx, 1, 2)
        above_row = jnp.where(first_row > 0, above_row, jnp.zeros_like(above_row))
        below_row = jnp.where(first_row + height < NX, below_row, jnp.zeros_like(below_row))
        rimmed = jnp.concatenate([above_row, middle, below_row], axis=2)
        operand = lax.optimization_barrier(derive(rimmed)).astype(jnp.float32)
        mixed = jnp.einsum("kim,mcrs->kicrs", weights, operand, precision=lax.Precision.HIGHEST)
        cond_part = lax.dynamic_slice_in_dim(cond, first_row, height, 1)
        expand_part = lax.dynamic_slice_in_dim(expand, first_row, height, 1)
        diffuse = jnp.sum(cond_part[:, None, None] * mixed[:, :, :nfield], axis=0)
        strain = jnp.sum(expand_part[:, None, None] * mixed[:, :, nfield:], axis=0)
        value = jnp.concatenate([diffuse[:, 0:1], diffuse[:, 1:3] - strain, diffuse[:, 3:]], axis=1)
        return lax.dynamic_update_slice_in_dim(result, value.astype(jnp.bfloat16), first_row, 2)

    start_value = jnp.zeros(fields.shape, jnp.bfloat16)
    return lax.fori_loop(0, NX // height, advance, start_value)
```

```python
import functools

import jax
import jax.numpy as jnp
from jax import lax
from jax.experimental import pallas as pl
from jax.experimental.pallas import tpu as pltpu
from jax.sharding import PartitionSpec as P

PAD_I = 24
SLOT = 24


def laid_out(blocks, dim):
    lengths = list(blocks.shape[1:])
    lengths[dim] *= blocks.shape[0]
    return jnp.moveaxis(blocks, 0, dim).reshape(lengths)


def copy_for_each(value, axis):
    copies = jnp.broadcast_to(value, (lax.axis_size(axis), *value.shape))
    return lax.all_to_all(copies, axis, split_axis=0, concat_axis=0, tiled=True)


def gather_directly(value, axis, dim):
    return laid_out(copy_for_each(value, axis), dim)


def edge_rows(cells, axis, dim):
    count = lax.axis_size(axis)
    ends = count - 1
    head = lax.slice_in_dim(cells, 0, 1, axis=dim)
    tail = lax.slice_in_dim(cells, cells.shape[dim] - 1, cells.shape[dim], axis=dim)
    above = lax.ppermute(tail, axis, [(i, (i + 1) % count) for i in range(ends)])
    below = lax.ppermute(head, axis, [((i + 1) % count, i) for i in range(ends)])
    return above, below


def kernel(nmode, nfield, rows, width, terms, nmat, nchar,
           fg_ref, top_ref, bot_ref, cp_ref, kl_ref, mat_ref, chr_ref,
           mt_ref, ct_ref, et_ref, out_ref, fs, os, cs, es):
    nloc = out_ref.shape[0]
    mat = mat_ref[...]
    chs = chr_ref[...]
    for k in range(terms):
        mv = jnp.zeros((rows, width), jnp.float32)
        ev = jnp.zeros((rows, width), jnp.float32)
        for m in range(nmat):
            hit = mat == m
            mv = jnp.where(hit, mt_ref[k, m], mv)
            ev = jnp.where(hit, et_ref[k, m], ev)
        cv = jnp.zeros((rows, width), jnp.float32)
        for q in range(nchar):
            cv = jnp.where(chs == q, ct_ref[k, q], cv)
        kl = kl_ref[k]
        cs[k] = kl * mv * cv
        es[k] = kl * ev

    def fill(jf, carry):
        src = pl.multiple_of(jf * rows, rows)
        dst = pl.multiple_of(jf * SLOT, 8)
        fs[pl.ds(dst, rows), :] = fg_ref[pl.ds(src, rows), :].astype(jnp.float32)
        return carry

    lax.fori_loop(0, nmode * nfield, fill, 0)
    fs[pl.ds(rows, nmode * nfield, stride=SLOT), :] = top_ref[...].astype(jnp.float32)
    fs[pl.ds(rows + 1, nmode * nfield, stride=SLOT), :] = bot_ref[...].astype(jnp.float32)

    lane = lax.broadcasted_iota(jnp.int32, (nmode, width), 1)
    first = lane == 0
    last = lane == width - 1
    stride = nfield * SLOT

    def row(f, r):
        return fs[pl.ds(f * SLOT + r, nmode, stride=stride), :]

    def step(x, carry):
        up = jnp.where(x == 0, rows, x - 1)
        down = jnp.where(x == rows - 1, rows + 1, x + 1)
        comps = []
        grads = None
        for f in range(nfield):
            center = row(f, x)
            above = row(f, up)
            below = row(f, down)
            left = jnp.where(first, 0.0, pltpu.roll(center, 1, 1))
            right = jnp.where(last, 0.0, pltpu.roll(center, width - 1, 1))
            lap = 4.0 * center - above - below - left - right
            comps.append(lap.astype(jnp.bfloat16))
            if f == 0:
                gx = 0.5 * (below - above)
                gy = 0.5 * (right - left)
                grads = (gx.astype(jnp.bfloat16), gy.astype(jnp.bfloat16))
        operand = jnp.concatenate(comps + list(grads), axis=1)
        mixed = jnp.dot(cp_ref[...], operand, preferred_element_type=jnp.float32)
        cvals = [jnp.broadcast_to(cs[k, pl.ds(x, 1), :], (PAD_I, width)) for k in range(terms)]
        evals = [jnp.broadcast_to(es[k, pl.ds(x, 1), :], (PAD_I, width)) for k in range(terms)]
        for f in range(nfield):
            diffuse = None
            for k in range(terms):
                part = cvals[k] * mixed[k * PAD_I:(k + 1) * PAD_I, f * width:(f + 1) * width]
                diffuse = part if diffuse is None else diffuse + part
            if f in (1, 2):
                c = nfield + f - 1
                strain = None
                for k in range(terms):
                    part = evals[k] * mixed[k * PAD_I:(k + 1) * PAD_I, c * width:(c + 1) * width]
                    strain = part if strain is None else strain + part
                diffuse = diffuse - strain
            os[pl.ds(f * rows + x, PAD_I, stride=nfield * rows), :] = diffuse
        return carry

    lax.fori_loop(0, rows, step, 0)

    def emit(i, carry):
        base = pl.multiple_of(i * nfield * rows, 8)
        out_ref[i] = os[pl.ds(base, nfield * rows), :].reshape(nfield, rows, width).astype(out_ref.dtype)
        return carry

    lax.fori_loop(0, nloc, emit, 0)


def body(
    fields, coupling, kl_field, material, char_state, material_table, char_table, expansion_table
):
    local_modes, nfield, rows, width = fields.shape
    terms = coupling.shape[0]
    total_modes = coupling.shape[1]
    gathered = gather_directly(fields, "modes", 0)
    above, below = edge_rows(gathered, "cells", 2)
    first_mode = lax.axis_index("modes") * local_modes
    weights = lax.dynamic_slice_in_dim(coupling, first_mode, local_modes, 1)
    weights = jnp.pad(weights, ((0, 0), (0, PAD_I - local_modes), (0, 0)))
    weights = weights.reshape(terms * PAD_I, total_modes)
    vmem = pl.BlockSpec(memory_space=pltpu.VMEM)
    smem = pl.BlockSpec(memory_space=pltpu.SMEM)
    run = pl.pallas_call(
        functools.partial(kernel, total_modes, nfield, rows, width, terms,
                          material_table.shape[1], char_table.shape[1]),
        out_shape=jax.ShapeDtypeStruct(fields.shape, fields.dtype),
        in_specs=[vmem] * 7 + [smem] * 3,
        out_specs=vmem,
        scratch_shapes=[
            pltpu.VMEM((total_modes * nfield * SLOT, width), jnp.float32),
            pltpu.VMEM((PAD_I * nfield * rows, width), jnp.float32),
            pltpu.VMEM((terms, rows, width), jnp.float32),
            pltpu.VMEM((terms, rows, width), jnp.float32),
        ],
        compiler_params=pltpu.CompilerParams(vmem_limit_bytes=48 * 1024 * 1024),
    )
    return run(
        gathered.reshape(total_modes * nfield * rows, width),
        above.reshape(total_modes * nfield, width),
        below.reshape(total_modes * nfield, width),
        weights,
        kl_field,
        material,
        char_state,
        material_table,
        char_table,
        expansion_table,
    )


def solution(mesh):
    return jax.shard_map(
        body,
        mesh=mesh,
        in_specs=(
            P("modes", None, "cells", None),
            P(),
            P(None, "cells", None),
            P("cells", None),
            P("cells", None),
            P(),
            P(),
            P(),
        ),
        out_specs=P("modes", None, "cells", None),
        check_vma=False,
    )
```

```python
import functools

import jax
import jax.numpy as jnp
from jax import lax
from jax.experimental import pallas as pl
from jax.experimental.pallas import tpu as pltpu
from jax.sharding import PartitionSpec as P

PAD_I = 24
SLOT = 24


def edge_rows(cells, axis, dim):
    count = lax.axis_size(axis)
    ends = count - 1
    head = lax.slice_in_dim(cells, 0, 1, axis=dim)
    tail = lax.slice_in_dim(cells, cells.shape[dim] - 1, cells.shape[dim], axis=dim)
    above = lax.ppermute(tail, axis, [(i, (i + 1) % count) for i in range(ends)])
    below = lax.ppermute(head, axis, [((i + 1) % count, i) for i in range(ends)])
    return above, below


def kernel(nmode, nfield, rows, width, terms, nmat, nchar,
           b0_ref, b1_ref, b2_ref, b3_ref, cp_ref, kl_ref, mat_ref, chr_ref,
           mt_ref, ct_ref, et_ref, out_ref, fs, os, cs, es):
    nloc = out_ref.shape[0]
    blocks = (b0_ref, b1_ref, b2_ref, b3_ref)
    mat = mat_ref[...]
    chs = chr_ref[...]
    for k in range(terms):
        mv = jnp.zeros((rows, width), jnp.float32)
        ev = jnp.zeros((rows, width), jnp.float32)
        for m in range(nmat):
            hit = mat == m
            mv = jnp.where(hit, mt_ref[k, m], mv)
            ev = jnp.where(hit, et_ref[k, m], ev)
        cv = jnp.zeros((rows, width), jnp.float32)
        for q in range(nchar):
            cv = jnp.where(chs == q, ct_ref[k, q], cv)
        kl = kl_ref[k]
        cs[k] = kl * mv * cv
        es[k] = kl * ev

    per = nloc * nfield
    for d, blk in enumerate(blocks):
        def fill(jf, carry, blk=blk, d=d):
            src = pl.multiple_of(jf * rows, rows)
            dst = pl.multiple_of((d * per + jf) * SLOT, 8)
            fs[pl.ds(dst, rows), :] = blk[pl.ds(src, rows), :].astype(jnp.float32)
            return carry

        lax.fori_loop(0, per, fill, 0, unroll=12)
        halo = per * rows
        fs[pl.ds(d * per * SLOT + rows, per, stride=SLOT), :] = blk[pl.ds(halo, per), :].astype(jnp.float32)
        fs[pl.ds(d * per * SLOT + rows + 1, per, stride=SLOT), :] = blk[pl.ds(halo + per, per), :].astype(jnp.float32)

    lane = lax.broadcasted_iota(jnp.int32, (nmode, width), 1)
    first = lane == 0
    last = lane == width - 1
    stride = nfield * SLOT

    def row(f, r):
        return fs[pl.ds(f * SLOT + r, nmode, stride=stride), :]

    def step(x, carry):
        up = jnp.where(x == 0, rows, x - 1)
        down = jnp.where(x == rows - 1, rows + 1, x + 1)
        comps = []
        grads = None
        for f in range(nfield):
            center = row(f, x)
            above = row(f, up)
            below = row(f, down)
            left = jnp.where(first, 0.0, pltpu.roll(center, 1, 1))
            right = jnp.where(last, 0.0, pltpu.roll(center, width - 1, 1))
            lap = 4.0 * center - above - below - left - right
            comps.append(lap.astype(jnp.bfloat16))
            if f == 0:
                gx = 0.5 * (below - above)
                gy = 0.5 * (right - left)
                grads = (gx.astype(jnp.bfloat16), gy.astype(jnp.bfloat16))
        operand = jnp.concatenate(comps + list(grads), axis=1)
        mixed = jnp.dot(cp_ref[...], operand, preferred_element_type=jnp.float32)
        cvals = [jnp.broadcast_to(cs[k, pl.ds(x, 1), :], (PAD_I, width)) for k in range(terms)]
        evals = [jnp.broadcast_to(es[k, pl.ds(x, 1), :], (PAD_I, width)) for k in range(terms)]
        for f in range(nfield):
            diffuse = None
            for k in range(terms):
                part = cvals[k] * mixed[k * PAD_I:(k + 1) * PAD_I, f * width:(f + 1) * width]
                diffuse = part if diffuse is None else diffuse + part
            if f in (1, 2):
                c = nfield + f - 1
                strain = None
                for k in range(terms):
                    part = evals[k] * mixed[k * PAD_I:(k + 1) * PAD_I, c * width:(c + 1) * width]
                    strain = part if strain is None else strain + part
                diffuse = diffuse - strain
            os[pl.ds(f * rows + x, PAD_I, stride=nfield * rows), :] = diffuse
        return carry

    lax.fori_loop(0, rows, step, 0)

    def emit(i, carry):
        base = pl.multiple_of(i * nfield * rows, 8)
        out_ref[i] = os[pl.ds(base, nfield * rows), :].reshape(nfield, rows, width).astype(out_ref.dtype)
        return carry

    lax.fori_loop(0, nloc, emit, 0)


def body(
    fields, coupling, kl_field, material, char_state, material_table, char_table, expansion_table
):
    local_modes, nfield, rows, width = fields.shape
    terms = coupling.shape[0]
    total_modes = coupling.shape[1]
    groups = lax.axis_size("modes")
    assert groups == 4
    above, below = edge_rows(fields, "cells", 2)
    pack = jnp.concatenate(
        [
            fields.reshape(local_modes * nfield * rows, width),
            above.reshape(local_modes * nfield, width),
            below.reshape(local_modes * nfield, width),
        ],
        axis=0,
    )
    partner = lax.ppermute(pack, "modes", [(i, i ^ 1) for i in range(groups)])
    counter = lax.ppermute(pack, "modes", [(i, i ^ 2) for i in range(groups)])
    diagonal = lax.ppermute(counter, "modes", [(i, i ^ 1) for i in range(groups)])
    me = lax.axis_index("modes")
    first_mode = me * local_modes
    weights = lax.dynamic_slice_in_dim(coupling, first_mode, local_modes, 1)
    weights = jnp.concatenate(
        [
            lax.dynamic_slice_in_dim(weights, (me ^ flip) * local_modes, local_modes, 2)
            for flip in range(groups)
        ],
        axis=2,
    )
    weights = jnp.pad(weights, ((0, 0), (0, PAD_I - local_modes), (0, 0)))
    weights = weights.reshape(terms * PAD_I, total_modes)
    vmem = pl.BlockSpec(memory_space=pltpu.VMEM)
    smem = pl.BlockSpec(memory_space=pltpu.SMEM)
    run = pl.pallas_call(
        functools.partial(kernel, total_modes, nfield, rows, width, terms,
                          material_table.shape[1], char_table.shape[1]),
        out_shape=jax.ShapeDtypeStruct(fields.shape, fields.dtype),
        in_specs=[vmem] * 8 + [smem] * 3,
        out_specs=vmem,
        scratch_shapes=[
            pltpu.VMEM((total_modes * nfield * SLOT, width), jnp.float32),
            pltpu.VMEM((PAD_I * nfield * rows, width), jnp.float32),
            pltpu.VMEM((terms, rows, width), jnp.float32),
            pltpu.VMEM((terms, rows, width), jnp.float32),
        ],
        compiler_params=pltpu.CompilerParams(vmem_limit_bytes=48 * 1024 * 1024),
    )
    return run(
        pack,
        partner,
        counter,
        diagonal,
        weights,
        kl_field,
        material,
        char_state,
        material_table,
        char_table,
        expansion_table,
    )


def solution(mesh):
    return jax.shard_map(
        body,
        mesh=mesh,
        in_specs=(
            P("modes", None, "cells", None),
            P(),
            P(None, "cells", None),
            P("cells", None),
            P("cells", None),
            P(),
            P(),
            P(),
        ),
        out_specs=P("modes", None, "cells", None),
        check_vma=False,
    )
```

```python
import functools

import jax
import jax.numpy as jnp
from jax import lax
from jax.experimental import pallas as pl
from jax.experimental.pallas import tpu as pltpu
from jax.sharding import PartitionSpec as P

PAD_I = 24
JS = 73
OS = 65


def edge_rows(cells, axis, dim):
    count = lax.axis_size(axis)
    ends = count - 1
    head = lax.slice_in_dim(cells, 0, 1, axis=dim)
    tail = lax.slice_in_dim(cells, cells.shape[dim] - 1, cells.shape[dim], axis=dim)
    above = lax.ppermute(tail, axis, [(i, (i + 1) % count) for i in range(ends)])
    below = lax.ppermute(head, axis, [((i + 1) % count, i) for i in range(ends)])
    return above, below


def kernel(nmode, nfield, rows, width, terms, nmat, nchar,
           b0_ref, b1_ref, b2_ref, b3_ref, cp_ref, kl_ref, mat_ref, chr_ref,
           mt_ref, ct_ref, et_ref, out_ref, fs, hs, os, cs, es):
    nloc = out_ref.shape[0]
    blocks = (b0_ref, b1_ref, b2_ref, b3_ref)
    mat = mat_ref[...]
    chs = chr_ref[...]
    for k in range(terms):
        mv = jnp.zeros((rows, width), jnp.float32)
        ev = jnp.zeros((rows, width), jnp.float32)
        for m in range(nmat):
            hit = mat == m
            mv = jnp.where(hit, mt_ref[k, m], mv)
            ev = jnp.where(hit, et_ref[k, m], ev)
        cv = jnp.zeros((rows, width), jnp.float32)
        for q in range(nchar):
            cv = jnp.where(chs == q, ct_ref[k, q], cv)
        kl = kl_ref[k]
        cs[k] = kl * mv * cv
        es[k] = kl * ev

    per = nloc * nfield
    core = nfield * rows
    for d, blk in enumerate(blocks):
        for jl in range(nloc):
            j = d * nloc + jl
            fs[pl.ds(j * JS, core), :] = blk[pl.ds(jl * core, core), :].astype(jnp.float32)
        hs[...] = blk[pl.ds(nloc * core, 2 * per), :].astype(jnp.float32)
        for side in range(2 * nfield):
            fs[pl.ds(d * nloc * JS + core + side, nloc, stride=JS), :] = hs[pl.ds(side * nloc, nloc), :]

    lane = lax.broadcasted_iota(jnp.int32, (nmode, width), 1)
    first = lane == 0
    last = lane == width - 1

    def row(r):
        return fs[pl.ds(r, nmode, stride=JS), :]

    def step(x, carry):
        comps = []
        grads = None
        for f in range(nfield):
            up = jnp.where(x == 0, core + 2 * f, f * rows + x - 1)
            down = jnp.where(x == rows - 1, core + 2 * f + 1, f * rows + x + 1)
            center = row(f * rows + x)
            above = row(up)
            below = row(down)
            left = jnp.where(first, 0.0, pltpu.roll(center, 1, 1))
            right = jnp.where(last, 0.0, pltpu.roll(center, width - 1, 1))
            lap = 4.0 * center - above - below - left - right
            comps.append(lap.astype(jnp.bfloat16))
            if f == 0:
                gx = 0.5 * (below - above)
                gy = 0.5 * (right - left)
                grads = (gx.astype(jnp.bfloat16), gy.astype(jnp.bfloat16))
        operand = jnp.concatenate(comps + list(grads), axis=1)
        mixed = jnp.dot(cp_ref[...], operand, preferred_element_type=jnp.float32)
        cvals = [jnp.broadcast_to(cs[k, pl.ds(x, 1), :], (PAD_I, width)) for k in range(terms)]
        evals = [jnp.broadcast_to(es[k, pl.ds(x, 1), :], (PAD_I, width)) for k in range(terms)]
        for f in range(nfield):
            diffuse = None
            for k in range(terms):
                part = cvals[k] * mixed[k * PAD_I:(k + 1) * PAD_I, f * width:(f + 1) * width]
                diffuse = part if diffuse is None else diffuse + part
            if f in (1, 2):
                c = nfield + f - 1
                strain = None
                for k in range(terms):
                    part = evals[k] * mixed[k * PAD_I:(k + 1) * PAD_I, c * width:(c + 1) * width]
                    strain = part if strain is None else strain + part
                diffuse = diffuse - strain
            os[pl.ds(f * rows + x, PAD_I, stride=OS), :] = diffuse
        return carry

    lax.fori_loop(0, rows, step, 0)

    for i in range(nloc):
        out_ref[i] = os[pl.ds(i * OS, core), :].reshape(nfield, rows, width).astype(out_ref.dtype)


def body(
    fields, coupling, kl_field, material, char_state, material_table, char_table, expansion_table
):
    local_modes, nfield, rows, width = fields.shape
    terms = coupling.shape[0]
    total_modes = coupling.shape[1]
    groups = lax.axis_size("modes")
    assert groups == 4
    above, below = edge_rows(fields, "cells", 2)
    pack = jnp.concatenate(
        [
            fields.reshape(local_modes * nfield * rows, width),
            jnp.stack([above[:, :, 0], below[:, :, 0]], axis=1)
            .transpose(2, 1, 0, 3)
            .reshape(2 * nfield * local_modes, width),
        ],
        axis=0,
    )
    partner = lax.ppermute(pack, "modes", [(i, i ^ 1) for i in range(groups)])
    counter = lax.ppermute(pack, "modes", [(i, i ^ 2) for i in range(groups)])
    diagonal = lax.ppermute(counter, "modes", [(i, i ^ 1) for i in range(groups)])
    me = lax.axis_index("modes")
    first_mode = me * local_modes
    weights = lax.dynamic_slice_in_dim(coupling, first_mode, local_modes, 1)
    weights = jnp.concatenate(
        [
            lax.dynamic_slice_in_dim(weights, (me ^ flip) * local_modes, local_modes, 2)
            for flip in range(groups)
        ],
        axis=2,
    )
    weights = jnp.pad(weights, ((0, 0), (0, PAD_I - local_modes), (0, 0)))
    weights = weights.reshape(terms * PAD_I, total_modes)
    vmem = pl.BlockSpec(memory_space=pltpu.VMEM)
    smem = pl.BlockSpec(memory_space=pltpu.SMEM)
    run = pl.pallas_call(
        functools.partial(kernel, total_modes, nfield, rows, width, terms,
                          material_table.shape[1], char_table.shape[1]),
        out_shape=jax.ShapeDtypeStruct(fields.shape, fields.dtype),
        in_specs=[vmem] * 8 + [smem] * 3,
        out_specs=vmem,
        scratch_shapes=[
            pltpu.VMEM((total_modes * JS, width), jnp.float32),
            pltpu.VMEM((2 * local_modes * nfield, width), jnp.float32),
            pltpu.VMEM((PAD_I * OS, width), jnp.float32),
            pltpu.VMEM((terms, rows, width), jnp.float32),
            pltpu.VMEM((terms, rows, width), jnp.float32),
        ],
        compiler_params=pltpu.CompilerParams(vmem_limit_bytes=48 * 1024 * 1024),
    )
    return run(
        pack,
        partner,
        counter,
        diagonal,
        weights,
        kl_field,
        material,
        char_state,
        material_table,
        char_table,
        expansion_table,
    )


def solution(mesh):
    return jax.shard_map(
        body,
        mesh=mesh,
        in_specs=(
            P("modes", None, "cells", None),
            P(),
            P(None, "cells", None),
            P("cells", None),
            P("cells", None),
            P(),
            P(),
            P(),
        ),
        out_specs=P("modes", None, "cells", None),
        check_vma=False,
    )
```

```python
import functools

import jax
import jax.numpy as jnp
from jax import lax
from jax.experimental import pallas as pl
from jax.experimental.pallas import tpu as pltpu
from jax.sharding import PartitionSpec as P


PAD_I = 24
JS = 73
OS = 65


def edge_rows(cells, axis, dim):
    count = lax.axis_size(axis)
    ends = count - 1
    head = lax.slice_in_dim(cells, 0, 1, axis=dim)
    tail = lax.slice_in_dim(cells, cells.shape[dim] - 1, cells.shape[dim], axis=dim)
    above = lax.ppermute(tail, axis, [(i, (i + 1) % count) for i in range(ends)])
    below = lax.ppermute(head, axis, [((i + 1) % count, i) for i in range(ends)])
    return above, below


def kernel(nblock, carried, nfield, rows, width, terms, nmat, nchar, *refs):
    blocks = refs[:nblock]
    cp_ref, kl_ref, mat_ref, chr_ref, mt_ref, ct_ref, et_ref = refs[nblock:nblock + 7]
    rest = refs[nblock + 7:]
    if carried:
        part_ref, rest = rest[0], rest[1:]
    out_ref, fs, hs, os, cs, es = rest
    nloc = out_ref.shape[0]
    nmode = nblock * nloc
    mat = mat_ref[...]
    chs = chr_ref[...]
    for k in range(terms):
        mv = jnp.zeros((rows, width), jnp.float32)
        ev = jnp.zeros((rows, width), jnp.float32)
        for m in range(nmat):
            hit = mat == m
            mv = jnp.where(hit, mt_ref[k, m], mv)
            ev = jnp.where(hit, et_ref[k, m], ev)
        cv = jnp.zeros((rows, width), jnp.float32)
        for q in range(nchar):
            cv = jnp.where(chs == q, ct_ref[k, q], cv)
        kl = kl_ref[k]
        cs[k] = kl * mv * cv
        es[k] = kl * ev

    per = nloc * nfield
    core = nfield * rows
    for d, blk in enumerate(blocks):
        for jl in range(nloc):
            j = d * nloc + jl
            fs[pl.ds(j * JS, core), :] = blk[pl.ds(jl * core, core), :].astype(jnp.float32)
        hs[...] = blk[pl.ds(nloc * core, 2 * per), :].astype(jnp.float32)
        for side in range(2 * nfield):
            fs[pl.ds(d * nloc * JS + core + side, nloc, stride=JS), :] = hs[pl.ds(side * nloc, nloc), :]

    lane = lax.broadcasted_iota(jnp.int32, (nmode, width), 1)
    first = lane == 0
    last = lane == width - 1

    def row(r):
        return fs[pl.ds(r, nmode, stride=JS), :]

    def step(x, carry):
        comps = []
        grads = None
        for f in range(nfield):
            up = jnp.where(x == 0, core + 2 * f, f * rows + x - 1)
            down = jnp.where(x == rows - 1, core + 2 * f + 1, f * rows + x + 1)
            center = row(f * rows + x)
            above = row(up)
            below = row(down)
            left = jnp.where(first, 0.0, pltpu.roll(center, 1, 1))
            right = jnp.where(last, 0.0, pltpu.roll(center, width - 1, 1))
            lap = 4.0 * center - above - below - left - right
            comps.append(lap.astype(jnp.bfloat16))
            if f == 0:
                gx = 0.5 * (below - above)
                gy = 0.5 * (right - left)
                grads = (gx.astype(jnp.bfloat16), gy.astype(jnp.bfloat16))
        operand = jnp.concatenate(comps + list(grads), axis=1)
        mixed = jnp.dot(cp_ref[...], operand, preferred_element_type=jnp.float32)
        cvals = [jnp.broadcast_to(cs[k, pl.ds(x, 1), :], (PAD_I, width)) for k in range(terms)]
        evals = [jnp.broadcast_to(es[k, pl.ds(x, 1), :], (PAD_I, width)) for k in range(terms)]
        for f in range(nfield):
            diffuse = None
            for k in range(terms):
                part = cvals[k] * mixed[k * PAD_I:(k + 1) * PAD_I, f * width:(f + 1) * width]
                diffuse = part if diffuse is None else diffuse + part
            if f in (1, 2):
                c = nfield + f - 1
                strain = None
                for k in range(terms):
                    part = evals[k] * mixed[k * PAD_I:(k + 1) * PAD_I, c * width:(c + 1) * width]
                    strain = part if strain is None else strain + part
                diffuse = diffuse - strain
            os[pl.ds(f * rows + x, PAD_I, stride=OS), :] = diffuse
        return carry

    lax.fori_loop(0, rows, step, 0, unroll=2)

    for i in range(nloc):
        value = os[pl.ds(i * OS, core), :].reshape(nfield, rows, width)
        if carried:
            value = value + part_ref[i]
        out_ref[i] = value.astype(out_ref.dtype)


def body(
    fields, coupling, kl_field, material, char_state, material_table, char_table, expansion_table
):
    local_modes, nfield, rows, width = fields.shape
    terms = coupling.shape[0]
    total_modes = coupling.shape[1]
    groups = lax.axis_size("modes")
    assert groups == 4
    above, below = edge_rows(fields, "cells", 2)
    pack = jnp.concatenate(
        [
            fields.reshape(local_modes * nfield * rows, width),
            jnp.stack([above[:, :, 0], below[:, :, 0]], axis=1)
            .transpose(2, 1, 0, 3)
            .reshape(2 * nfield * local_modes, width),
        ],
        axis=0,
    )
    partner = lax.ppermute(pack, "modes", [(i, i ^ 1) for i in range(groups)])
    counter = lax.ppermute(pack, "modes", [(i, i ^ 2) for i in range(groups)])
    diagonal = lax.ppermute(counter, "modes", [(i, i ^ 1) for i in range(groups)])
    me = lax.axis_index("modes")
    first_mode = me * local_modes
    weights = lax.dynamic_slice_in_dim(coupling, first_mode, local_modes, 1)
    weights = jnp.concatenate(
        [
            lax.dynamic_slice_in_dim(weights, (me ^ flip) * local_modes, local_modes, 2)
            for flip in range(groups)
        ],
        axis=2,
    )
    weights = jnp.pad(weights, ((0, 0), (0, PAD_I - local_modes), (0, 0)))
    weights = weights.reshape(terms * PAD_I, total_modes)
    vmem = pl.BlockSpec(memory_space=pltpu.VMEM)
    smem = pl.BlockSpec(memory_space=pltpu.SMEM)
    half = groups // 2
    tables = (kl_field, material, char_state, material_table, char_table, expansion_table)

    def stage(packs, cols, partial, dtype):
        nblock = len(packs)
        nmode = nblock * local_modes
        flops = 2 * terms * PAD_I * nmode * (nfield + 2) * rows * width
        run = pl.pallas_call(
            functools.partial(kernel, nblock, partial is not None, nfield, rows, width, terms,
                              material_table.shape[1], char_table.shape[1]),
            out_shape=jax.ShapeDtypeStruct(fields.shape, dtype),
            in_specs=[vmem] * (nblock + 4) + [smem] * 3 + ([vmem] if partial is not None else []),
            out_specs=vmem,
            scratch_shapes=[
                pltpu.VMEM((nmode * JS, width), jnp.float32),
                pltpu.VMEM((2 * local_modes * nfield, width), jnp.float32),
                pltpu.VMEM((PAD_I * OS, width), jnp.float32),
                pltpu.VMEM((terms, rows, width), jnp.float32),
                pltpu.VMEM((terms, rows, width), jnp.float32),
            ],
            compiler_params=pltpu.CompilerParams(vmem_limit_bytes=48 * 1024 * 1024),
            cost_estimate=pl.CostEstimate(
                flops=flops, transcendentals=0, bytes_accessed=nblock * pack.size * 2 + fields.size * 6
            ),
        )
        extra = () if partial is None else (partial,)
        return run(*packs, cols, *tables, *extra)

    first = stage((pack, partner), weights[:, : half * local_modes], None, jnp.float32)
    return stage((counter, diagonal), weights[:, half * local_modes:], first, fields.dtype)


def solution(mesh):
    return jax.shard_map(
        body,
        mesh=mesh,
        in_specs=(
            P("modes", None, "cells", None),
            P(),
            P(None, "cells", None),
            P("cells", None),
            P("cells", None),
            P(),
            P(),
            P(),
        ),
        out_specs=P("modes", None, "cells", None),
        check_vma=False,
    )
```

```python
import functools

import jax
import jax.numpy as jnp
from jax import lax
from jax.experimental import pallas as pl
from jax.experimental.pallas import tpu as pltpu
from jax.sharding import PartitionSpec as P


PAD_I = 24
JS = 73
OS = 65


def edge_rows(cells, axis, dim):
    count = lax.axis_size(axis)
    ends = count - 1
    head = lax.slice_in_dim(cells, 0, 1, axis=dim)
    tail = lax.slice_in_dim(cells, cells.shape[dim] - 1, cells.shape[dim], axis=dim)
    above = lax.ppermute(tail, axis, [(i, (i + 1) % count) for i in range(ends)])
    below = lax.ppermute(head, axis, [((i + 1) % count, i) for i in range(ends)])
    return above, below


def kernel(nblock, final, nfield, rows, width, terms, nmat, nchar, *refs):
    blocks = refs[:nblock]
    if final:
        prev_ref, cp_ref, kl_ref, mat_ref, chr_ref, mt_ref, ct_ref, et_ref = refs[nblock:nblock + 8]
        out_ref, fs, hs, os, cs, es = refs[nblock + 8:]
        nloc = out_ref.shape[0]
    else:
        out_ref, fs, hs = refs[nblock:]
    nloc = blocks[0].shape[0] // (nfield * (rows + 2))
    nmode = nblock * nloc
    span = fs.shape[0] // JS
    core = nfield * rows
    per = nloc * nfield

    if final:
        mat = mat_ref[...]
        chs = chr_ref[...]
        for k in range(terms):
            mv = jnp.zeros((rows, width), jnp.float32)
            ev = jnp.zeros((rows, width), jnp.float32)
            for m in range(nmat):
                hit = mat == m
                mv = jnp.where(hit, mt_ref[k, m], mv)
                ev = jnp.where(hit, et_ref[k, m], ev)
            cv = jnp.zeros((rows, width), jnp.float32)
            for q in range(nchar):
                cv = jnp.where(chs == q, ct_ref[k, q], cv)
            kl = kl_ref[k]
            cs[k] = kl * mv * cv
            es[k] = kl * ev

    for d, blk in enumerate(blocks):
        for jl in range(nloc):
            j = d * nloc + jl
            fs[pl.ds(j * JS, core), :] = blk[pl.ds(jl * core, core), :].astype(jnp.float32)
        hs[...] = blk[pl.ds(nloc * core, 2 * per), :].astype(jnp.float32)
        for side in range(2 * nfield):
            fs[pl.ds(d * nloc * JS + core + side, nloc, stride=JS), :] = hs[pl.ds(side * nloc, nloc), :]
    if span > nmode:
        fs[pl.ds(nmode * JS, (span - nmode) * JS), :] = jnp.zeros(((span - nmode) * JS, width), jnp.float32)

    lane = lax.broadcasted_iota(jnp.int32, (span, width), 1)
    first = lane == 0
    last = lane == width - 1

    def row(r):
        return fs[pl.ds(r, span, stride=JS), :]

    def derive(x):
        comps = []
        grads = None
        for f in range(nfield):
            up = jnp.where(x == 0, core + 2 * f, f * rows + x - 1)
            down = jnp.where(x == rows - 1, core + 2 * f + 1, f * rows + x + 1)
            center = row(f * rows + x)
            above = row(up)
            below = row(down)
            left = jnp.where(first, 0.0, pltpu.roll(center, 1, 1))
            right = jnp.where(last, 0.0, pltpu.roll(center, width - 1, 1))
            lap = 4.0 * center - above - below - left - right
            comps.append(lap.astype(jnp.bfloat16))
            if f == 0:
                gx = 0.5 * (below - above)
                gy = 0.5 * (right - left)
                grads = (gx.astype(jnp.bfloat16), gy.astype(jnp.bfloat16))
        return jnp.concatenate(comps + list(grads), axis=1)

    if not final:
        def keep(x, carry):
            out_ref[x] = derive(x)
            return carry

        lax.fori_loop(0, rows, keep, 0, unroll=8)
        return

    def step(x, carry):
        operand = jnp.concatenate([prev_ref[x], derive(x)], axis=0)
        mixed = jnp.dot(cp_ref[...], operand, preferred_element_type=jnp.float32)
        cvals = [jnp.broadcast_to(cs[k, pl.ds(x, 1), :], (PAD_I, width)) for k in range(terms)]
        evals = [jnp.broadcast_to(es[k, pl.ds(x, 1), :], (PAD_I, width)) for k in range(terms)]
        for f in range(nfield):
            diffuse = None
            for k in range(terms):
                part = cvals[k] * mixed[k * PAD_I:(k + 1) * PAD_I, f * width:(f + 1) * width]
                diffuse = part if diffuse is None else diffuse + part
            if f in (1, 2):
                c = nfield + f - 1
                strain = None
                for k in range(terms):
                    part = evals[k] * mixed[k * PAD_I:(k + 1) * PAD_I, c * width:(c + 1) * width]
                    strain = part if strain is None else strain + part
                diffuse = diffuse - strain
            os[pl.ds(f * rows + x, PAD_I, stride=OS), :] = diffuse
        return carry

    lax.fori_loop(0, rows, step, 0, unroll=16)

    for i in range(out_ref.shape[0]):
        out_ref[i] = os[pl.ds(i * OS, core), :].reshape(nfield, rows, width).astype(out_ref.dtype)


def body(
    fields, coupling, kl_field, material, char_state, material_table, char_table, expansion_table
):
    local_modes, nfield, rows, width = fields.shape
    terms = coupling.shape[0]
    total_modes = coupling.shape[1]
    groups = lax.axis_size("modes")
    assert groups == 4
    above, below = edge_rows(fields, "cells", 2)
    pack = jnp.concatenate(
        [
            fields.reshape(local_modes * nfield * rows, width),
            jnp.stack([above[:, :, 0], below[:, :, 0]], axis=1)
            .transpose(2, 1, 0, 3)
            .reshape(2 * nfield * local_modes, width),
        ],
        axis=0,
    )
    partner = lax.ppermute(pack, "modes", [(i, i ^ 1) for i in range(groups)])
    counter = lax.ppermute(pack, "modes", [(i, i ^ 2) for i in range(groups)])
    diagonal = lax.ppermute(counter, "modes", [(i, i ^ 1) for i in range(groups)])
    me = lax.axis_index("modes")
    first_mode = me * local_modes
    weights = lax.dynamic_slice_in_dim(coupling, first_mode, local_modes, 1)
    weights = jnp.concatenate(
        [
            lax.dynamic_slice_in_dim(weights, (me ^ flip) * local_modes, local_modes, 2)
            for flip in range(groups)
        ],
        axis=2,
    )
    weights = jnp.pad(weights, ((0, 0), (0, PAD_I - local_modes), (0, 0)))
    vmem = pl.BlockSpec(memory_space=pltpu.VMEM)
    smem = pl.BlockSpec(memory_space=pltpu.SMEM)
    half = groups // 2
    span = -(-half * local_modes // 16) * 16
    tables = (kl_field, material, char_state, material_table, char_table, expansion_table)
    gap = span - half * local_modes
    weights = weights.reshape(terms, PAD_I, total_modes)
    zeros = jnp.zeros((terms, PAD_I, gap), weights.dtype)
    cols = jnp.concatenate(
        [weights[:, :, : half * local_modes], zeros, weights[:, :, half * local_modes:], zeros], axis=2
    ).reshape(terms * PAD_I, 2 * span)
    comps = nfield + 2
    scratch = [
        pltpu.VMEM((span * JS, width), jnp.float32),
        pltpu.VMEM((2 * local_modes * nfield, width), jnp.float32),
    ]
    params = pltpu.CompilerParams(vmem_limit_bytes=48 * 1024 * 1024)

    ops = pl.pallas_call(
        functools.partial(kernel, half, False, nfield, rows, width, terms,
                          material_table.shape[1], char_table.shape[1]),
        out_shape=jax.ShapeDtypeStruct((rows, span, comps * width), jnp.bfloat16),
        in_specs=[vmem] * half,
        out_specs=vmem,
        scratch_shapes=scratch,
        compiler_params=params,
        cost_estimate=pl.CostEstimate(
            flops=12 * span * comps * rows * width, transcendentals=0,
            bytes_accessed=half * pack.size * 2 + rows * span * comps * width * 2,
        ),
    )(pack, partner)
    return pl.pallas_call(
        functools.partial(kernel, half, True, nfield, rows, width, terms,
                          material_table.shape[1], char_table.shape[1]),
        out_shape=jax.ShapeDtypeStruct(fields.shape, fields.dtype),
        in_specs=[vmem] * (half + 5) + [smem] * 3,
        out_specs=vmem,
        scratch_shapes=scratch + [
            pltpu.VMEM((PAD_I * OS, width), jnp.float32),
            pltpu.VMEM((terms, rows, width), jnp.float32),
            pltpu.VMEM((terms, rows, width), jnp.float32),
        ],
        compiler_params=params,
        cost_estimate=pl.CostEstimate(
            flops=2 * terms * PAD_I * 2 * span * comps * rows * width, transcendentals=0,
            bytes_accessed=half * pack.size * 2 + rows * span * comps * width * 2 + fields.size * 2,
        ),
    )(counter, diagonal, ops, cols, *tables)


def solution(mesh):
    return jax.shard_map(
        body,
        mesh=mesh,
        in_specs=(
            P("modes", None, "cells", None),
            P(),
            P(None, "cells", None),
            P("cells", None),
            P("cells", None),
            P(),
            P(),
            P(),
        ),
        out_specs=P("modes", None, "cells", None),
        check_vma=False,
    )
```

```python
import functools

import jax
import jax.numpy as jnp
from jax import lax
from jax.experimental import pallas as pl
from jax.experimental.pallas import tpu as pltpu
from jax.sharding import PartitionSpec as P


PAD_I = 24
JS = 73
OS = 65


def edge_rows(cells, axis, dim):
    count = lax.axis_size(axis)
    ends = count - 1
    head = lax.slice_in_dim(cells, 0, 1, axis=dim)
    tail = lax.slice_in_dim(cells, cells.shape[dim] - 1, cells.shape[dim], axis=dim)
    above = lax.ppermute(tail, axis, [(i, (i + 1) % count) for i in range(ends)])
    below = lax.ppermute(head, axis, [((i + 1) % count, i) for i in range(ends)])
    return above, below


def kernel(nblock, prev, final, partial, nfield, rows, width, terms, nmat, nchar, *refs):
    blocks = refs[:nblock]
    refs = refs[nblock:]
    if prev:
        prev_ref, refs = refs[0], refs[1:]
    if final:
        cp_ref, kl_ref, mat_ref, chr_ref, mt_ref, ct_ref, et_ref = refs[:7]
        refs = refs[7:]
        if partial:
            part_ref, refs = refs[0], refs[1:]
        out_ref, fs, hs, os, cs, es = refs
    else:
        out_ref, fs, hs = refs
    nloc = blocks[0].shape[0] // (nfield * (rows + 2))
    nmode = nblock * nloc
    span = fs.shape[0] // JS
    core = nfield * rows
    per = nloc * nfield

    if final:
        mat = mat_ref[...]
        chs = chr_ref[...]
        for k in range(terms):
            mv = jnp.zeros((rows, width), jnp.float32)
            ev = jnp.zeros((rows, width), jnp.float32)
            for m in range(nmat):
                hit = mat == m
                mv = jnp.where(hit, mt_ref[k, m], mv)
                ev = jnp.where(hit, et_ref[k, m], ev)
            cv = jnp.zeros((rows, width), jnp.float32)
            for q in range(nchar):
                cv = jnp.where(chs == q, ct_ref[k, q], cv)
            kl = kl_ref[k]
            cs[k] = kl * mv * cv
            es[k] = kl * ev

    for d, blk in enumerate(blocks):
        for jl in range(nloc):
            j = d * nloc + jl
            fs[pl.ds(j * JS, core), :] = blk[pl.ds(jl * core, core), :].astype(jnp.float32)
        hs[...] = blk[pl.ds(nloc * core, 2 * per), :].astype(jnp.float32)
        for side in range(2 * nfield):
            fs[pl.ds(d * nloc * JS + core + side, nloc, stride=JS), :] = hs[pl.ds(side * nloc, nloc), :]
    if span > nmode:
        fs[pl.ds(nmode * JS, (span - nmode) * JS), :] = jnp.zeros(((span - nmode) * JS, width), jnp.float32)

    lane = lax.broadcasted_iota(jnp.int32, (span, width), 1)
    first = lane == 0
    last = lane == width - 1

    def row(r):
        return fs[pl.ds(r, span, stride=JS), :]

    def derive(x):
        comps = []
        grads = None
        for f in range(nfield):
            up = jnp.where(x == 0, core + 2 * f, f * rows + x - 1)
            down = jnp.where(x == rows - 1, core + 2 * f + 1, f * rows + x + 1)
            center = row(f * rows + x)
            above = row(up)
            below = row(down)
            left = jnp.where(first, 0.0, pltpu.roll(center, 1, 1))
            right = jnp.where(last, 0.0, pltpu.roll(center, width - 1, 1))
            lap = 4.0 * center - above - below - left - right
            comps.append(lap.astype(jnp.bfloat16))
            if f == 0:
                gx = 0.5 * (below - above)
                gy = 0.5 * (right - left)
                grads = (gx.astype(jnp.bfloat16), gy.astype(jnp.bfloat16))
        return jnp.concatenate(comps + list(grads), axis=1)

    if not final:
        def keep(x, carry):
            out_ref[x] = derive(x)
            return carry

        lax.fori_loop(0, rows, keep, 0, unroll=8)
        return

    def step(x, carry):
        operand = derive(x)
        if prev:
            operand = jnp.concatenate([prev_ref[x], operand], axis=0)
        mixed = jnp.dot(cp_ref[...], operand, preferred_element_type=jnp.float32)
        cvals = [jnp.broadcast_to(cs[k, pl.ds(x, 1), :], (PAD_I, width)) for k in range(terms)]
        evals = [jnp.broadcast_to(es[k, pl.ds(x, 1), :], (PAD_I, width)) for k in range(terms)]
        for f in range(nfield):
            diffuse = None
            for k in range(terms):
                part = cvals[k] * mixed[k * PAD_I:(k + 1) * PAD_I, f * width:(f + 1) * width]
                diffuse = part if diffuse is None else diffuse + part
            if f in (1, 2):
                c = nfield + f - 1
                strain = None
                for k in range(terms):
                    part = evals[k] * mixed[k * PAD_I:(k + 1) * PAD_I, c * width:(c + 1) * width]
                    strain = part if strain is None else strain + part
                diffuse = diffuse - strain
            os[pl.ds(f * rows + x, PAD_I, stride=OS), :] = diffuse
        return carry

    lax.fori_loop(0, rows, step, 0, unroll=16)

    for i in range(out_ref.shape[0]):
        value = os[pl.ds(i * OS, core), :].reshape(nfield, rows, width)
        if partial:
            value = value + part_ref[i]
        out_ref[i] = value.astype(out_ref.dtype)


def body(
    fields, coupling, kl_field, material, char_state, material_table, char_table, expansion_table
):
    local_modes, nfield, rows, width = fields.shape
    terms = coupling.shape[0]
    groups = lax.axis_size("modes")
    assert groups == 4
    above, below = edge_rows(fields, "cells", 2)
    pack = jnp.concatenate(
        [
            fields.reshape(local_modes * nfield * rows, width),
            jnp.stack([above[:, :, 0], below[:, :, 0]], axis=1)
            .transpose(2, 1, 0, 3)
            .reshape(2 * nfield * local_modes, width),
        ],
        axis=0,
    )
    partner = lax.ppermute(pack, "modes", [(i, i ^ 1) for i in range(groups)])
    counter = lax.ppermute(pack, "modes", [(i, i ^ 2) for i in range(groups)])
    diagonal = lax.ppermute(counter, "modes", [(i, i ^ 1) for i in range(groups)])
    me = lax.axis_index("modes")
    first_mode = me * local_modes
    weights = lax.dynamic_slice_in_dim(coupling, first_mode, local_modes, 1)
    weights = jnp.concatenate(
        [
            lax.dynamic_slice_in_dim(weights, (me ^ flip) * local_modes, local_modes, 2)
            for flip in range(groups)
        ],
        axis=2,
    )
    weights = jnp.pad(weights, ((0, 0), (0, PAD_I - local_modes), (0, 0)))
    vmem = pl.BlockSpec(memory_space=pltpu.VMEM)
    smem = pl.BlockSpec(memory_space=pltpu.SMEM)
    tables = (kl_field, material, char_state, material_table, char_table, expansion_table)
    comps = nfield + 2
    params = pltpu.CompilerParams(vmem_limit_bytes=48 * 1024 * 1024)
    nmat, nchar = material_table.shape[1], char_table.shape[1]

    def padded(count):
        return -(-count * local_modes // 16) * 16

    def columns(groups_of_blocks):
        pieces = []
        for lo, hi in groups_of_blocks:
            pieces.append(weights[:, :, lo * local_modes:hi * local_modes])
            gap = padded(hi - lo) - (hi - lo) * local_modes
            if gap:
                pieces.append(jnp.zeros((terms, PAD_I, gap), weights.dtype))
        cat = jnp.concatenate(pieces, axis=2)
        return cat.reshape(terms * PAD_I, cat.shape[2])

    def scratch(count):
        return [
            pltpu.VMEM((padded(count) * JS, width), jnp.float32),
            pltpu.VMEM((2 * local_modes * nfield, width), jnp.float32),
        ]

    mix_scratch = [
        pltpu.VMEM((PAD_I * OS, width), jnp.float32),
        pltpu.VMEM((terms, rows, width), jnp.float32),
        pltpu.VMEM((terms, rows, width), jnp.float32),
    ]

    def mix_cost(span):
        return pl.CostEstimate(
            flops=2 * terms * PAD_I * span * comps * rows * width, transcendentals=0,
            bytes_accessed=span * comps * rows * width * 2 + fields.size * 8,
        )

    partial = pl.pallas_call(
        functools.partial(kernel, 2, False, True, False, nfield, rows, width, terms, nmat, nchar),
        out_shape=jax.ShapeDtypeStruct(fields.shape, jnp.float32),
        in_specs=[vmem] * 6 + [smem] * 3,
        out_specs=vmem,
        scratch_shapes=scratch(2) + mix_scratch,
        compiler_params=params,
        cost_estimate=mix_cost(padded(2)),
    )(pack, partner, columns([(0, 2)]), *tables)
    ops = pl.pallas_call(
        functools.partial(kernel, 1, False, False, False, nfield, rows, width, terms, nmat, nchar),
        out_shape=jax.ShapeDtypeStruct((rows, padded(1), comps * width), jnp.bfloat16),
        in_specs=[vmem],
        out_specs=vmem,
        scratch_shapes=scratch(1),
        compiler_params=params,
        cost_estimate=pl.CostEstimate(
            flops=12 * padded(1) * comps * rows * width, transcendentals=0,
            bytes_accessed=pack.size * 2 + rows * padded(1) * comps * width * 2,
        ),
    )(counter)
    return pl.pallas_call(
        functools.partial(kernel, 1, True, True, True, nfield, rows, width, terms, nmat, nchar),
        out_shape=jax.ShapeDtypeStruct(fields.shape, fields.dtype),
        in_specs=[vmem] * 6 + [smem] * 3 + [vmem],
        out_specs=vmem,
        scratch_shapes=scratch(1) + mix_scratch,
        compiler_params=params,
        cost_estimate=mix_cost(2 * padded(1)),
    )(diagonal, ops, columns([(2, 3), (3, 4)]), *tables, partial)


def solution(mesh):
    return jax.shard_map(
        body,
        mesh=mesh,
        in_specs=(
            P("modes", None, "cells", None),
            P(),
            P(None, "cells", None),
            P("cells", None),
            P("cells", None),
            P(),
            P(),
            P(),
        ),
        out_specs=P("modes", None, "cells", None),
        check_vma=False,
    )
```

```python
import functools

import jax
import jax.numpy as jnp
from jax import lax
from jax.experimental import pallas as pl
from jax.experimental.pallas import tpu as pltpu
from jax.sharding import PartitionSpec as P


PAD_I = 24
JS = 73
OS = 65


def edge_rows(cells, axis, dim):
    count = lax.axis_size(axis)
    ends = count - 1
    head = lax.slice_in_dim(cells, 0, 1, axis=dim)
    tail = lax.slice_in_dim(cells, cells.shape[dim] - 1, cells.shape[dim], axis=dim)
    above = lax.ppermute(tail, axis, [(i, (i + 1) % count) for i in range(ends)])
    below = lax.ppermute(head, axis, [((i + 1) % count, i) for i in range(ends)])
    return above, below


def kernel(nblock, prev, final, partial, nfield, rows, width, terms, nmat, nchar, *refs):
    blocks = [(refs[2 * b], refs[2 * b + 1]) for b in range(nblock)]
    refs = refs[2 * nblock:]
    if prev:
        prev_ref, refs = refs[0], refs[1:]
    if final:
        cp_ref, kl_ref, mat_ref, chr_ref, mt_ref, ct_ref, et_ref = refs[:7]
        refs = refs[7:]
        if partial:
            part_ref, refs = refs[0], refs[1:]
        out_ref, fs, hs, os, cs, es = refs
    else:
        out_ref, fs, hs = refs
    nloc = blocks[0][0].shape[0] // (nfield * rows)
    nmode = nblock * nloc
    span = fs.shape[0] // JS
    core = nfield * rows

    if final:
        mat = mat_ref[...]
        chs = chr_ref[...]
        for k in range(terms):
            mv = jnp.zeros((rows, width), jnp.float32)
            ev = jnp.zeros((rows, width), jnp.float32)
            for m in range(nmat):
                hit = mat == m
                mv = jnp.where(hit, mt_ref[k, m], mv)
                ev = jnp.where(hit, et_ref[k, m], ev)
            cv = jnp.zeros((rows, width), jnp.float32)
            for q in range(nchar):
                cv = jnp.where(chs == q, ct_ref[k, q], cv)
            kl = kl_ref[k]
            cs[k] = kl * mv * cv
            es[k] = kl * ev

    for d, (blk, hal) in enumerate(blocks):
        for jl in range(nloc):
            j = d * nloc + jl
            fs[pl.ds(j * JS, core), :] = blk[pl.ds(jl * core, core), :].astype(jnp.float32)
        hs[...] = hal[...].astype(jnp.float32)
        for side in range(2 * nfield):
            fs[pl.ds(d * nloc * JS + core + side, nloc, stride=JS), :] = hs[pl.ds(side * nloc, nloc), :]
    if span > nmode:
        fs[pl.ds(nmode * JS, (span - nmode) * JS), :] = jnp.zeros(((span - nmode) * JS, width), jnp.float32)

    lane = lax.broadcasted_iota(jnp.int32, (span, width), 1)
    first = lane == 0
    last = lane == width - 1

    def row(r):
        return fs[pl.ds(r, span, stride=JS), :]

    def derive(x):
        comps = []
        grads = None
        for f in range(nfield):
            up = jnp.where(x == 0, core + 2 * f, f * rows + x - 1)
            down = jnp.where(x == rows - 1, core + 2 * f + 1, f * rows + x + 1)
            center = row(f * rows + x)
            above = row(up)
            below = row(down)
            left = jnp.where(first, 0.0, pltpu.roll(center, 1, 1))
            right = jnp.where(last, 0.0, pltpu.roll(center, width - 1, 1))
            lap = 4.0 * center - above - below - left - right
            comps.append(lap.astype(jnp.bfloat16))
            if f == 0:
                gx = 0.5 * (below - above)
                gy = 0.5 * (right - left)
                grads = (gx.astype(jnp.bfloat16), gy.astype(jnp.bfloat16))
        return jnp.concatenate(comps + list(grads), axis=1)

    if not final:
        def keep(x, carry):
            out_ref[x] = derive(x)
            return carry

        lax.fori_loop(0, rows, keep, 0, unroll=8)
        return

    def step(x, carry):
        operand = derive(x)
        if prev:
            operand = jnp.concatenate([prev_ref[x], operand], axis=0)
        mixed = jnp.dot(cp_ref[...], operand, preferred_element_type=jnp.float32)
        cvals = [jnp.broadcast_to(cs[k, pl.ds(x, 1), :], (PAD_I, width)) for k in range(terms)]
        evals = [jnp.broadcast_to(es[k, pl.ds(x, 1), :], (PAD_I, width)) for k in range(terms)]
        for f in range(nfield):
            diffuse = None
            for k in range(terms):
                part = cvals[k] * mixed[k * PAD_I:(k + 1) * PAD_I, f * width:(f + 1) * width]
                diffuse = part if diffuse is None else diffuse + part
            if f in (1, 2):
                c = nfield + f - 1
                strain = None
                for k in range(terms):
                    part = evals[k] * mixed[k * PAD_I:(k + 1) * PAD_I, c * width:(c + 1) * width]
                    strain = part if strain is None else strain + part
                diffuse = diffuse - strain
            os[pl.ds(f * rows + x, PAD_I, stride=OS), :] = diffuse
        return carry

    lax.fori_loop(0, rows, step, 0, unroll=16)

    for i in range(out_ref.shape[0]):
        value = os[pl.ds(i * OS, core), :].reshape(nfield, rows, width)
        if partial:
            value = value + part_ref[i]
        out_ref[i] = value.astype(out_ref.dtype)


def body(
    fields, coupling, kl_field, material, char_state, material_table, char_table, expansion_table
):
    local_modes, nfield, rows, width = fields.shape
    terms = coupling.shape[0]
    groups = lax.axis_size("modes")
    assert groups == 4
    cells = fields.reshape(local_modes * nfield * rows, width)
    counter = lax.ppermute(cells, "modes", [(i, i ^ 2) for i in range(groups)])
    partner = lax.ppermute(cells, "modes", [(i, i ^ 1) for i in range(groups)])
    above, below = edge_rows(fields, "cells", 2)
    halo = (
        jnp.stack([above[:, :, 0], below[:, :, 0]], axis=1)
        .transpose(2, 1, 0, 3)
        .reshape(2 * nfield * local_modes, width)
    )
    counter_halo = lax.ppermute(halo, "modes", [(i, i ^ 2) for i in range(groups)])
    partner_halo = lax.ppermute(halo, "modes", [(i, i ^ 1) for i in range(groups)])
    diagonal, diagonal_halo = lax.ppermute(
        (counter, counter_halo), "modes", [(i, i ^ 1) for i in range(groups)]
    )
    me = lax.axis_index("modes")
    first_mode = me * local_modes
    weights = lax.dynamic_slice_in_dim(coupling, first_mode, local_modes, 1)
    weights = jnp.concatenate(
        [
            lax.dynamic_slice_in_dim(weights, (me ^ flip) * local_modes, local_modes, 2)
            for flip in range(groups)
        ],
        axis=2,
    )
    weights = jnp.pad(weights, ((0, 0), (0, PAD_I - local_modes), (0, 0)))
    vmem = pl.BlockSpec(memory_space=pltpu.VMEM)
    smem = pl.BlockSpec(memory_space=pltpu.SMEM)
    tables = (kl_field, material, char_state, material_table, char_table, expansion_table)
    comps = nfield + 2
    params = pltpu.CompilerParams(vmem_limit_bytes=48 * 1024 * 1024)
    nmat, nchar = material_table.shape[1], char_table.shape[1]

    def padded(count):
        return -(-count * local_modes // 16) * 16

    def columns(groups_of_blocks):
        pieces = []
        for lo, hi in groups_of_blocks:
            pieces.append(weights[:, :, lo * local_modes:hi * local_modes])
            gap = padded(hi - lo) - (hi - lo) * local_modes
            if gap:
                pieces.append(jnp.zeros((terms, PAD_I, gap), weights.dtype))
        cat = jnp.concatenate(pieces, axis=2)
        return cat.reshape(terms * PAD_I, cat.shape[2])

    def scratch(count):
        return [
            pltpu.VMEM((padded(count) * JS, width), jnp.float32),
            pltpu.VMEM((2 * local_modes * nfield, width), jnp.float32),
        ]

    mix_scratch = [
        pltpu.VMEM((PAD_I * OS, width), jnp.float32),
        pltpu.VMEM((terms, rows, width), jnp.float32),
        pltpu.VMEM((terms, rows, width), jnp.float32),
    ]

    def mix_cost(span):
        return pl.CostEstimate(
            flops=2 * terms * PAD_I * span * comps * rows * width, transcendentals=0,
            bytes_accessed=span * comps * rows * width * 2 + fields.size * 8,
        )

    partial = pl.pallas_call(
        functools.partial(kernel, 2, False, True, False, nfield, rows, width, terms, nmat, nchar),
        out_shape=jax.ShapeDtypeStruct(fields.shape, jnp.float32),
        in_specs=[vmem] * 8 + [smem] * 3,
        out_specs=vmem,
        scratch_shapes=scratch(2) + mix_scratch,
        compiler_params=params,
        cost_estimate=mix_cost(padded(2)),
    )(cells, halo, partner, partner_halo, columns([(0, 2)]), *tables)
    ops = pl.pallas_call(
        functools.partial(kernel, 1, False, False, False, nfield, rows, width, terms, nmat, nchar),
        out_shape=jax.ShapeDtypeStruct((rows, padded(1), comps * width), jnp.bfloat16),
        in_specs=[vmem] * 2,
        out_specs=vmem,
        scratch_shapes=scratch(1),
        compiler_params=params,
        cost_estimate=pl.CostEstimate(
            flops=12 * padded(1) * comps * rows * width, transcendentals=0,
            bytes_accessed=fields.size * 2 + rows * padded(1) * comps * width * 2,
        ),
    )(counter, counter_halo)
    return pl.pallas_call(
        functools.partial(kernel, 1, True, True, True, nfield, rows, width, terms, nmat, nchar),
        out_shape=jax.ShapeDtypeStruct(fields.shape, fields.dtype),
        in_specs=[vmem] * 7 + [smem] * 3 + [vmem],
        out_specs=vmem,
        scratch_shapes=scratch(1) + mix_scratch,
        compiler_params=params,
        cost_estimate=mix_cost(2 * padded(1)),
    )(diagonal, diagonal_halo, ops, columns([(2, 3), (3, 4)]), *tables, partial)


def solution(mesh):
    return jax.shard_map(
        body,
        mesh=mesh,
        in_specs=(
            P("modes", None, "cells", None),
            P(),
            P(None, "cells", None),
            P("cells", None),
            P("cells", None),
            P(),
            P(),
            P(),
        ),
        out_specs=P("modes", None, "cells", None),
        check_vma=False,
    )
```

```python
import functools

import jax
import jax.numpy as jnp
from jax import lax
from jax.experimental import pallas as pl
from jax.experimental.pallas import tpu as pltpu
from jax.sharding import PartitionSpec as P


PAD_I = 24
JS = 73
EDGE = 96
OS = 65


def edges_kernel(rows, count, x_ref, head_ref, tail_ref, xs):
    xs[...] = x_ref[...].astype(jnp.float32)
    spare = head_ref.shape[0] - count
    gap = jnp.zeros((spare, head_ref.shape[1]), jnp.float32)
    head = xs[pl.ds(0, count, stride=rows), :]
    tail = xs[pl.ds(rows - 1, count, stride=rows), :]
    head_ref[...] = jnp.concatenate([head, gap], axis=0).astype(head_ref.dtype)
    tail_ref[...] = jnp.concatenate([tail, gap], axis=0).astype(tail_ref.dtype)


def edge_rows(cells, axis):
    count = lax.axis_size(axis)
    ends = count - 1
    local_modes, nfield, rows, width = cells.shape
    blocks = local_modes * nfield
    vmem = pl.BlockSpec(memory_space=pltpu.VMEM)
    head, tail = pl.pallas_call(
        functools.partial(edges_kernel, rows, blocks),
        out_shape=(jax.ShapeDtypeStruct((EDGE, width), cells.dtype),) * 2,
        in_specs=[vmem],
        out_specs=(vmem, vmem),
        scratch_shapes=[pltpu.VMEM((blocks * rows, width), jnp.float32)],
    )(cells.reshape(blocks * rows, width))
    above = lax.ppermute(tail, axis, [(i, (i + 1) % count) for i in range(ends)])
    below = lax.ppermute(head, axis, [((i + 1) % count, i) for i in range(ends)])
    return above, below


def kernel(nblock, prev, final, partial, nfield, rows, width, terms, nmat, nchar, *refs):
    blocks = refs[:nblock]
    refs = refs[nblock:]
    if prev:
        prev_ref, refs = refs[0], refs[1:]
    if final:
        cp_ref, kl_ref, mat_ref, chr_ref, mt_ref, ct_ref, et_ref = refs[:7]
        refs = refs[7:]
        if partial:
            part_ref, refs = refs[0], refs[1:]
        out_ref, fs, hs, os, cs, es = refs
    else:
        out_ref, fs, hs = refs
    nloc = (blocks[0].shape[0] - 2 * EDGE) // (nfield * rows)
    nmode = nblock * nloc
    span = fs.shape[0] // JS
    core = nfield * rows

    if final:
        mat = mat_ref[...]
        chs = chr_ref[...]
        for k in range(terms):
            mv = jnp.zeros((rows, width), jnp.float32)
            ev = jnp.zeros((rows, width), jnp.float32)
            for m in range(nmat):
                hit = mat == m
                mv = jnp.where(hit, mt_ref[k, m], mv)
                ev = jnp.where(hit, et_ref[k, m], ev)
            cv = jnp.zeros((rows, width), jnp.float32)
            for q in range(nchar):
                cv = jnp.where(chs == q, ct_ref[k, q], cv)
            kl = kl_ref[k]
            cs[k] = kl * mv * cv
            es[k] = kl * ev

    for d, blk in enumerate(blocks):
        for jl in range(nloc):
            j = d * nloc + jl
            fs[pl.ds(j * JS, core), :] = blk[pl.ds(jl * core, core), :].astype(jnp.float32)
        hs[...] = blk[pl.ds(nloc * core, 2 * EDGE), :].astype(jnp.float32)
        for side in range(2):
            for f in range(nfield):
                fs[pl.ds(d * nloc * JS + core + 2 * f + side, nloc, stride=JS), :] = hs[
                    pl.ds(side * EDGE + f, nloc, stride=nfield), :
                ]
    if span > nmode:
        fs[pl.ds(nmode * JS, (span - nmode) * JS), :] = jnp.zeros(((span - nmode) * JS, width), jnp.float32)

    lane = lax.broadcasted_iota(jnp.int32, (span, width), 1)
    first = lane == 0
    last = lane == width - 1

    def row(r):
        return fs[pl.ds(r, span, stride=JS), :]

    def derive(x):
        comps = []
        grads = None
        for f in range(nfield):
            up = jnp.where(x == 0, core + 2 * f, f * rows + x - 1)
            down = jnp.where(x == rows - 1, core + 2 * f + 1, f * rows + x + 1)
            center = row(f * rows + x)
            above = row(up)
            below = row(down)
            left = jnp.where(first, 0.0, pltpu.roll(center, 1, 1))
            right = jnp.where(last, 0.0, pltpu.roll(center, width - 1, 1))
            lap = 4.0 * center - above - below - left - right
            comps.append(lap.astype(jnp.bfloat16))
            if f == 0:
                gx = 0.5 * (below - above)
                gy = 0.5 * (right - left)
                grads = (gx.astype(jnp.bfloat16), gy.astype(jnp.bfloat16))
        return jnp.concatenate(comps + list(grads), axis=1)

    if not final:
        def keep(x, carry):
            out_ref[x] = derive(x)
            return carry

        lax.fori_loop(0, rows, keep, 0, unroll=8)
        return

    def step(x, carry):
        operand = derive(x)
        if prev:
            operand = jnp.concatenate([prev_ref[x], operand], axis=0)
        mixed = jnp.dot(cp_ref[...], operand, preferred_element_type=jnp.float32)
        cvals = [jnp.broadcast_to(cs[k, pl.ds(x, 1), :], (PAD_I, width)) for k in range(terms)]
        evals = [jnp.broadcast_to(es[k, pl.ds(x, 1), :], (PAD_I, width)) for k in range(terms)]
        for f in range(nfield):
            diffuse = None
            for k in range(terms):
                part = cvals[k] * mixed[k * PAD_I:(k + 1) * PAD_I, f * width:(f + 1) * width]
                diffuse = part if diffuse is None else diffuse + part
            if f in (1, 2):
                c = nfield + f - 1
                strain = None
                for k in range(terms):
                    part = evals[k] * mixed[k * PAD_I:(k + 1) * PAD_I, c * width:(c + 1) * width]
                    strain = part if strain is None else strain + part
                diffuse = diffuse - strain
            os[pl.ds(f * rows + x, PAD_I, stride=OS), :] = diffuse
        return carry

    lax.fori_loop(0, rows, step, 0, unroll=16)

    for i in range(out_ref.shape[0]):
        value = os[pl.ds(i * OS, core), :].reshape(nfield, rows, width)
        if partial:
            value = value + part_ref[i]
        out_ref[i] = value.astype(out_ref.dtype)


def body(
    fields, coupling, kl_field, material, char_state, material_table, char_table, expansion_table
):
    local_modes, nfield, rows, width = fields.shape
    terms = coupling.shape[0]
    groups = lax.axis_size("modes")
    assert groups == 4
    above, below = edge_rows(fields, "cells")
    pack = jnp.concatenate(
        [
            fields.reshape(local_modes * nfield * rows, width),
            above,
            below,
        ],
        axis=0,
    )
    partner = lax.ppermute(pack, "modes", [(i, i ^ 1) for i in range(groups)])
    counter = lax.ppermute(pack, "modes", [(i, i ^ 2) for i in range(groups)])
    diagonal = lax.ppermute(counter, "modes", [(i, i ^ 1) for i in range(groups)])
    me = lax.axis_index("modes")
    first_mode = me * local_modes
    weights = lax.dynamic_slice_in_dim(coupling, first_mode, local_modes, 1)
    weights = jnp.concatenate(
        [
            lax.dynamic_slice_in_dim(weights, (me ^ flip) * local_modes, local_modes, 2)
            for flip in range(groups)
        ],
        axis=2,
    )
    weights = jnp.pad(weights, ((0, 0), (0, PAD_I - local_modes), (0, 0)))
    vmem = pl.BlockSpec(memory_space=pltpu.VMEM)
    smem = pl.BlockSpec(memory_space=pltpu.SMEM)
    tables = (kl_field, material, char_state, material_table, char_table, expansion_table)
    comps = nfield + 2
    params = pltpu.CompilerParams(vmem_limit_bytes=48 * 1024 * 1024)
    nmat, nchar = material_table.shape[1], char_table.shape[1]

    def padded(count):
        return -(-count * local_modes // 16) * 16

    def columns(groups_of_blocks):
        pieces = []
        for lo, hi in groups_of_blocks:
            pieces.append(weights[:, :, lo * local_modes:hi * local_modes])
            gap = padded(hi - lo) - (hi - lo) * local_modes
            if gap:
                pieces.append(jnp.zeros((terms, PAD_I, gap), weights.dtype))
        cat = jnp.concatenate(pieces, axis=2)
        return cat.reshape(terms * PAD_I, cat.shape[2])

    def scratch(count):
        return [
            pltpu.VMEM((padded(count) * JS, width), jnp.float32),
            pltpu.VMEM((2 * EDGE, width), jnp.float32),
        ]

    mix_scratch = [
        pltpu.VMEM((PAD_I * OS, width), jnp.float32),
        pltpu.VMEM((terms, rows, width), jnp.float32),
        pltpu.VMEM((terms, rows, width), jnp.float32),
    ]

    def mix_cost(span):
        return pl.CostEstimate(
            flops=2 * terms * PAD_I * span * comps * rows * width, transcendentals=0,
            bytes_accessed=span * comps * rows * width * 2 + fields.size * 8,
        )

    partial = pl.pallas_call(
        functools.partial(kernel, 2, False, True, False, nfield, rows, width, terms, nmat, nchar),
        out_shape=jax.ShapeDtypeStruct(fields.shape, jnp.float32),
        in_specs=[vmem] * 6 + [smem] * 3,
        out_specs=vmem,
        scratch_shapes=scratch(2) + mix_scratch,
        compiler_params=params,
        cost_estimate=mix_cost(padded(2)),
    )(pack, partner, columns([(0, 2)]), *tables)
    ops = pl.pallas_call(
        functools.partial(kernel, 1, False, False, False, nfield, rows, width, terms, nmat, nchar),
        out_shape=jax.ShapeDtypeStruct((rows, padded(1), comps * width), jnp.bfloat16),
        in_specs=[vmem],
        out_specs=vmem,
        scratch_shapes=scratch(1),
        compiler_params=params,
        cost_estimate=pl.CostEstimate(
            flops=12 * padded(1) * comps * rows * width, transcendentals=0,
            bytes_accessed=pack.size * 2 + rows * padded(1) * comps * width * 2,
        ),
    )(counter)
    return pl.pallas_call(
        functools.partial(kernel, 1, True, True, True, nfield, rows, width, terms, nmat, nchar),
        out_shape=jax.ShapeDtypeStruct(fields.shape, fields.dtype),
        in_specs=[vmem] * 6 + [smem] * 3 + [vmem],
        out_specs=vmem,
        scratch_shapes=scratch(1) + mix_scratch,
        compiler_params=params,
        cost_estimate=mix_cost(2 * padded(1)),
    )(diagonal, ops, columns([(2, 3), (3, 4)]), *tables, partial)


def solution(mesh):
    return jax.shard_map(
        body,
        mesh=mesh,
        in_specs=(
            P("modes", None, "cells", None),
            P(),
            P(None, "cells", None),
            P("cells", None),
            P("cells", None),
            P(),
            P(),
            P(),
        ),
        out_specs=P("modes", None, "cells", None),
        check_vma=False,
    )
```

```python
import functools

import jax
import jax.numpy as jnp
from jax import lax
from jax.experimental import pallas as pl
from jax.experimental.pallas import tpu as pltpu
from jax.sharding import PartitionSpec as P


PAD_I = 24
JS = 73
OS = 65


def kernel(nblock, prev, final, partial, nfield, rows, width, terms, nmat, nchar, *refs):
    blocks = refs[:nblock]
    refs = refs[nblock:]
    if prev:
        prev_ref, refs = refs[0], refs[1:]
    if final:
        cp_ref, kl_ref, mat_ref, chr_ref, mt_ref, ct_ref, et_ref = refs[:7]
        refs = refs[7:]
        if partial:
            part_ref, refs = refs[0], refs[1:]
        out_ref, edge_ref, fs, hs, os, cs, es = refs
    else:
        out_ref, edge_ref, fs, hs = refs
    nloc = blocks[0].shape[0] // (nfield * rows)
    nmode = nblock * nloc
    span = fs.shape[0] // JS
    core = nfield * rows

    if final:
        mat = mat_ref[...]
        chs = chr_ref[...]
        for k in range(terms):
            mv = jnp.zeros((rows, width), jnp.float32)
            ev = jnp.zeros((rows, width), jnp.float32)
            for m in range(nmat):
                hit = mat == m
                mv = jnp.where(hit, mt_ref[k, m], mv)
                ev = jnp.where(hit, et_ref[k, m], ev)
            cv = jnp.zeros((rows, width), jnp.float32)
            for q in range(nchar):
                cv = jnp.where(chs == q, ct_ref[k, q], cv)
            kl = kl_ref[k]
            cs[k] = kl * mv * cv
            es[k] = kl * ev

    for d, blk in enumerate(blocks):
        for jl in range(nloc):
            j = d * nloc + jl
            fs[pl.ds(j * JS, core), :] = blk[pl.ds(jl * core, core), :].astype(jnp.float32)
    if span > nmode:
        fs[pl.ds(nmode * JS, (span - nmode) * JS), :] = jnp.zeros(((span - nmode) * JS, width), jnp.float32)

    lane = lax.broadcasted_iota(jnp.int32, (span, width), 1)
    first = lane == 0
    last = lane == width - 1

    def row(r):
        return fs[pl.ds(r, span, stride=JS), :]

    for e, r in enumerate((0, 1, rows - 2, rows - 1)):
        for f in range(nfield):
            edge_ref[e, f] = row(f * rows + r).astype(edge_ref.dtype)

    def derive(x):
        comps = []
        grads = None
        for f in range(nfield):
            up = f * rows + x - 1
            down = f * rows + x + 1
            center = row(f * rows + x)
            above = row(up)
            below = row(down)
            left = jnp.where(first, 0.0, pltpu.roll(center, 1, 1))
            right = jnp.where(last, 0.0, pltpu.roll(center, width - 1, 1))
            lap = 4.0 * center - above - below - left - right
            comps.append(lap.astype(jnp.bfloat16))
            if f == 0:
                gx = 0.5 * (below - above)
                gy = 0.5 * (right - left)
                grads = (gx.astype(jnp.bfloat16), gy.astype(jnp.bfloat16))
        return jnp.concatenate(comps + list(grads), axis=1)

    if not final:
        def keep(x, carry):
            out_ref[x] = derive(x)
            return carry

        lax.fori_loop(1, rows - 1, keep, 0, unroll=7)
        return

    def step(x, carry):
        operand = derive(x)
        if prev:
            operand = jnp.concatenate([prev_ref[x], operand], axis=0)
        mixed = jnp.dot(cp_ref[...], operand, preferred_element_type=jnp.float32)
        cvals = [jnp.broadcast_to(cs[k, pl.ds(x, 1), :], (PAD_I, width)) for k in range(terms)]
        evals = [jnp.broadcast_to(es[k, pl.ds(x, 1), :], (PAD_I, width)) for k in range(terms)]
        for f in range(nfield):
            diffuse = None
            for k in range(terms):
                part = cvals[k] * mixed[k * PAD_I:(k + 1) * PAD_I, f * width:(f + 1) * width]
                diffuse = part if diffuse is None else diffuse + part
            if f in (1, 2):
                c = nfield + f - 1
                strain = None
                for k in range(terms):
                    part = evals[k] * mixed[k * PAD_I:(k + 1) * PAD_I, c * width:(c + 1) * width]
                    strain = part if strain is None else strain + part
                diffuse = diffuse - strain
            os[pl.ds(f * rows + x, PAD_I, stride=OS), :] = diffuse
        return carry

    lax.fori_loop(1, rows - 1, step, 0, unroll=14)

    for i in range(out_ref.shape[0]):
        value = os[pl.ds(i * OS, core), :].reshape(nfield, rows, width)
        if partial:
            value = value + part_ref[i]
        out_ref[i] = value.astype(out_ref.dtype)


def edge_kernel(nfield, rows, width, terms, nmat, nchar, e1, e2, e3, up_ref, down_ref, cp_ref, kl_ref,
                mat_ref, chr_ref, mt_ref, ct_ref, et_ref, inner_ref, out_ref):
    mat = mat_ref[...]
    chs = chr_ref[...]
    cond, expand = [], []
    for k in range(terms):
        mv = jnp.zeros((rows, width), jnp.float32)
        ev = jnp.zeros((rows, width), jnp.float32)
        for m in range(nmat):
            hit = mat == m
            mv = jnp.where(hit, mt_ref[k, m], mv)
            ev = jnp.where(hit, et_ref[k, m], ev)
        cv = jnp.zeros((rows, width), jnp.float32)
        for q in range(nchar):
            cv = jnp.where(chs == q, ct_ref[k, q], cv)
        kl = kl_ref[k]
        cond.append(kl * mv * cv)
        expand.append(kl * ev)
    pieces = (e1, e2, e3)

    def gather(e, f):
        return jnp.concatenate([p[e, f] for p in pieces], axis=0).astype(jnp.float32)

    span = sum(p.shape[2] for p in pieces)
    lane = lax.broadcasted_iota(jnp.int32, (span, width), 1)
    first = lane == 0
    last = lane == width - 1
    results = {}
    for x, e_mid, e_in, outer in ((0, 0, 1, up_ref), (rows - 1, 3, 2, down_ref)):
        comps = []
        grads = None
        for f in range(nfield):
            center = gather(e_mid, f)
            inner = gather(e_in, f)
            edge = outer[f].astype(jnp.float32)
            above, below = (edge, inner) if x == 0 else (inner, edge)
            left = jnp.where(first, 0.0, pltpu.roll(center, 1, 1))
            right = jnp.where(last, 0.0, pltpu.roll(center, width - 1, 1))
            lap = 4.0 * center - above - below - left - right
            comps.append(lap.astype(jnp.bfloat16))
            if f == 0:
                gx = 0.5 * (below - above)
                gy = 0.5 * (right - left)
                grads = (gx.astype(jnp.bfloat16), gy.astype(jnp.bfloat16))
        operand = jnp.concatenate(comps + list(grads), axis=1)
        mixed = jnp.dot(cp_ref[...], operand, preferred_element_type=jnp.float32)
        cvals = [jnp.broadcast_to(cond[k][x:x + 1, :], (PAD_I, width)) for k in range(terms)]
        evals = [jnp.broadcast_to(expand[k][x:x + 1, :], (PAD_I, width)) for k in range(terms)]
        for f in range(nfield):
            diffuse = None
            for k in range(terms):
                part = cvals[k] * mixed[k * PAD_I:(k + 1) * PAD_I, f * width:(f + 1) * width]
                diffuse = part if diffuse is None else diffuse + part
            if f in (1, 2):
                c = nfield + f - 1
                strain = None
                for k in range(terms):
                    part = evals[k] * mixed[k * PAD_I:(k + 1) * PAD_I, c * width:(c + 1) * width]
                    strain = part if strain is None else strain + part
                diffuse = diffuse - strain
            results[(x, f)] = diffuse
    row = lax.broadcasted_iota(jnp.int32, (rows, width), 0)
    for i in range(out_ref.shape[0]):
        for f in range(nfield):
            value = inner_ref[i, f]
            value = jnp.where(row == 0, jnp.broadcast_to(results[(0, f)][i:i + 1, :], (rows, width)), value)
            value = jnp.where(
                row == rows - 1, jnp.broadcast_to(results[(rows - 1, f)][i:i + 1, :], (rows, width)), value
            )
            out_ref[i, f] = value.astype(out_ref.dtype)


def body(
    fields, coupling, kl_field, material, char_state, material_table, char_table, expansion_table
):
    local_modes, nfield, rows, width = fields.shape
    terms = coupling.shape[0]
    groups = lax.axis_size("modes")
    assert groups == 4
    cells = fields.reshape(local_modes * nfield * rows, width)
    counter = lax.ppermute(cells, "modes", [(i, i ^ 2) for i in range(groups)])
    partner = lax.ppermute(cells, "modes", [(i, i ^ 1) for i in range(groups)])
    diagonal = lax.ppermute(counter, "modes", [(i, i ^ 1) for i in range(groups)])
    me = lax.axis_index("modes")
    first_mode = me * local_modes
    weights = lax.dynamic_slice_in_dim(coupling, first_mode, local_modes, 1)
    weights = jnp.concatenate(
        [
            lax.dynamic_slice_in_dim(weights, (me ^ flip) * local_modes, local_modes, 2)
            for flip in range(groups)
        ],
        axis=2,
    )
    weights = jnp.pad(weights, ((0, 0), (0, PAD_I - local_modes), (0, 0)))
    vmem = pl.BlockSpec(memory_space=pltpu.VMEM)
    smem = pl.BlockSpec(memory_space=pltpu.SMEM)
    tables = (kl_field, material, char_state, material_table, char_table, expansion_table)
    comps = nfield + 2
    params = pltpu.CompilerParams(vmem_limit_bytes=48 * 1024 * 1024)
    nmat, nchar = material_table.shape[1], char_table.shape[1]

    def padded(count):
        return -(-count * local_modes // 16) * 16

    def columns(groups_of_blocks):
        pieces = []
        for lo, hi in groups_of_blocks:
            pieces.append(weights[:, :, lo * local_modes:hi * local_modes])
            gap = padded(hi - lo) - (hi - lo) * local_modes
            if gap:
                pieces.append(jnp.zeros((terms, PAD_I, gap), weights.dtype))
        cat = jnp.concatenate(pieces, axis=2)
        return cat.reshape(terms * PAD_I, cat.shape[2])

    def scratch(count):
        return [
            pltpu.VMEM((padded(count) * JS, width), jnp.float32),
            pltpu.VMEM((8, width), jnp.float32),
        ]

    def edge_shape(count):
        return jax.ShapeDtypeStruct((4, nfield, padded(count), width), fields.dtype)

    mix_scratch = [
        pltpu.VMEM((PAD_I * OS, width), jnp.float32),
        pltpu.VMEM((terms, rows, width), jnp.float32),
        pltpu.VMEM((terms, rows, width), jnp.float32),
    ]

    def mix_cost(span):
        return pl.CostEstimate(
            flops=2 * terms * PAD_I * span * comps * rows * width, transcendentals=0,
            bytes_accessed=span * comps * rows * width * 2 + fields.size * 8,
        )

    partial, e1 = pl.pallas_call(
        functools.partial(kernel, 2, False, True, False, nfield, rows, width, terms, nmat, nchar),
        out_shape=(jax.ShapeDtypeStruct(fields.shape, jnp.float32), edge_shape(2)),
        in_specs=[vmem] * 6 + [smem] * 3,
        out_specs=(vmem, vmem),
        scratch_shapes=scratch(2) + mix_scratch,
        compiler_params=params,
        cost_estimate=mix_cost(padded(2)),
    )(cells, partner, columns([(0, 2)]), *tables)
    ops, e2 = pl.pallas_call(
        functools.partial(kernel, 1, False, False, False, nfield, rows, width, terms, nmat, nchar),
        out_shape=(jax.ShapeDtypeStruct((rows, padded(1), comps * width), jnp.bfloat16), edge_shape(1)),
        in_specs=[vmem],
        out_specs=(vmem, vmem),
        scratch_shapes=scratch(1),
        compiler_params=params,
        cost_estimate=pl.CostEstimate(
            flops=12 * padded(1) * comps * rows * width, transcendentals=0,
            bytes_accessed=cells.size * 2 + rows * padded(1) * comps * width * 2,
        ),
    )(counter)
    run = pl.pallas_call(
        functools.partial(kernel, 1, True, True, True, nfield, rows, width, terms, nmat, nchar),
        out_shape=(jax.ShapeDtypeStruct(fields.shape, jnp.float32), edge_shape(1)),
        in_specs=[vmem] * 6 + [smem] * 3 + [vmem],
        out_specs=(vmem, vmem),
        scratch_shapes=scratch(1) + mix_scratch,
        compiler_params=params,
        cost_estimate=mix_cost(2 * padded(1)),
    )
    inner, e3 = run(diagonal, ops, columns([(2, 3), (3, 4)]), *tables, partial)
    head = jnp.concatenate([e1[0], e2[0], e3[0]], axis=1)
    tail = jnp.concatenate([e1[3], e2[3], e3[3]], axis=1)
    count = lax.axis_size("cells")
    above = lax.ppermute(tail, "cells", [(i, i + 1) for i in range(count - 1)])
    below = lax.ppermute(head, "cells", [(i + 1, i) for i in range(count - 1)])
    return pl.pallas_call(
        functools.partial(edge_kernel, nfield, rows, width, terms, nmat, nchar),
        out_shape=jax.ShapeDtypeStruct(fields.shape, fields.dtype),
        in_specs=[vmem] * 9 + [smem] * 3 + [vmem],
        out_specs=vmem,
        compiler_params=params,
    )(e1, e2, e3, above, below, columns([(0, 2), (2, 3), (3, 4)]), *tables, inner)


def solution(mesh):
    return jax.shard_map(
        body,
        mesh=mesh,
        in_specs=(
            P("modes", None, "cells", None),
            P(),
            P(None, "cells", None),
            P("cells", None),
            P("cells", None),
            P(),
            P(),
            P(),
        ),
        out_specs=P("modes", None, "cells", None),
        check_vma=False,
    )
```

```python
import functools

import jax
import jax.numpy as jnp
from jax import lax
from jax.experimental import pallas as pl
from jax.experimental.pallas import tpu as pltpu
from jax.sharding import PartitionSpec as P


PAD_I = 24
JS = 73
OS = 65


def edge_rows(cells, axis, dim):
    count = lax.axis_size(axis)
    ends = count - 1
    head = lax.slice_in_dim(cells, 0, 1, axis=dim)
    tail = lax.slice_in_dim(cells, cells.shape[dim] - 1, cells.shape[dim], axis=dim)
    above = lax.ppermute(tail, axis, [(i, (i + 1) % count) for i in range(ends)])
    below = lax.ppermute(head, axis, [((i + 1) % count, i) for i in range(ends)])
    return above, below


def kernel(nblock, prev, final, partial, make, nfield, rows, width, terms, nmat, nchar, *refs):
    blocks = refs[:nblock]
    refs = refs[nblock:]
    if prev:
        prev_ref, refs = refs[0], refs[1:]
    if final and make:
        cp_ref, kl_ref, mat_ref, chr_ref, mt_ref, ct_ref, et_ref = refs[:7]
        refs = refs[7:]
        if partial:
            part_ref, refs = refs[0], refs[1:]
        out_ref, cs, es, fs, hs, os = refs
    elif final:
        cp_ref, cs, es = refs[:3]
        refs = refs[3:]
        if partial:
            part_ref, refs = refs[0], refs[1:]
        out_ref, fs, hs, os = refs
    else:
        out_ref, fs, hs = refs
    nloc = blocks[0].shape[0] // (nfield * (rows + 2))
    nmode = nblock * nloc
    span = fs.shape[0] // JS
    core = nfield * rows
    per = nloc * nfield

    if final and make:
        mat = mat_ref[...]
        chs = chr_ref[...]
        for k in range(terms):
            mv = jnp.zeros((rows, width), jnp.float32)
            ev = jnp.zeros((rows, width), jnp.float32)
            for m in range(nmat):
                hit = mat == m
                mv = jnp.where(hit, mt_ref[k, m], mv)
                ev = jnp.where(hit, et_ref[k, m], ev)
            cv = jnp.zeros((rows, width), jnp.float32)
            for q in range(nchar):
                cv = jnp.where(chs == q, ct_ref[k, q], cv)
            kl = kl_ref[k]
            cs[k] = kl * mv * cv
            es[k] = kl * ev

    for d, blk in enumerate(blocks):
        for jl in range(nloc):
            j = d * nloc + jl
            fs[pl.ds(j * JS, core), :] = blk[pl.ds(jl * core, core), :].astype(jnp.float32)
        hs[...] = blk[pl.ds(nloc * core, 2 * per), :].astype(jnp.float32)
        for side in range(2 * nfield):
            fs[pl.ds(d * nloc * JS + core + side, nloc, stride=JS), :] = hs[pl.ds(side * nloc, nloc), :]
    if span > nmode:
        fs[pl.ds(nmode * JS, (span - nmode) * JS), :] = jnp.zeros(((span - nmode) * JS, width), jnp.float32)

    lane = lax.broadcasted_iota(jnp.int32, (span, width), 1)
    first = lane == 0
    last = lane == width - 1

    def row(r):
        return fs[pl.ds(r, span, stride=JS), :]

    def derive(x):
        comps = []
        grads = None
        for f in range(nfield):
            up = jnp.where(x == 0, core + 2 * f, f * rows + x - 1)
            down = jnp.where(x == rows - 1, core + 2 * f + 1, f * rows + x + 1)
            center = row(f * rows + x)
            above = row(up)
            below = row(down)
            left = jnp.where(first, 0.0, pltpu.roll(center, 1, 1))
            right = jnp.where(last, 0.0, pltpu.roll(center, width - 1, 1))
            lap = 4.0 * center - above - below - left - right
            comps.append(lap.astype(jnp.bfloat16))
            if f == 0:
                gx = 0.5 * (below - above)
                gy = 0.5 * (right - left)
                grads = (gx.astype(jnp.bfloat16), gy.astype(jnp.bfloat16))
        return jnp.concatenate(comps + list(grads), axis=1)

    if not final:
        def keep(x, carry):
            out_ref[x] = derive(x)
            return carry

        lax.fori_loop(0, rows, keep, 0, unroll=8)
        return

    def step(x, carry):
        operand = derive(x)
        if prev:
            operand = jnp.concatenate([prev_ref[x], operand], axis=0)
        mixed = jnp.dot(cp_ref[...], operand, preferred_element_type=jnp.float32)
        cvals = [jnp.broadcast_to(cs[k, pl.ds(x, 1), :], (PAD_I, width)) for k in range(terms)]
        evals = [jnp.broadcast_to(es[k, pl.ds(x, 1), :], (PAD_I, width)) for k in range(terms)]
        for f in range(nfield):
            diffuse = None
            for k in range(terms):
                part = cvals[k] * mixed[k * PAD_I:(k + 1) * PAD_I, f * width:(f + 1) * width]
                diffuse = part if diffuse is None else diffuse + part
            if f in (1, 2):
                c = nfield + f - 1
                strain = None
                for k in range(terms):
                    part = evals[k] * mixed[k * PAD_I:(k + 1) * PAD_I, c * width:(c + 1) * width]
                    strain = part if strain is None else strain + part
                diffuse = diffuse - strain
            os[pl.ds(f * rows + x, PAD_I, stride=OS), :] = diffuse
        return carry

    lax.fori_loop(0, rows, step, 0, unroll=16)

    for i in range(out_ref.shape[0]):
        value = os[pl.ds(i * OS, core), :].reshape(nfield, rows, width)
        if partial:
            value = value + part_ref[i]
        out_ref[i] = value.astype(out_ref.dtype)


def body(
    fields, coupling, kl_field, material, char_state, material_table, char_table, expansion_table
):
    local_modes, nfield, rows, width = fields.shape
    terms = coupling.shape[0]
    groups = lax.axis_size("modes")
    assert groups == 4
    above, below = edge_rows(fields, "cells", 2)
    pack = jnp.concatenate(
        [
            fields.reshape(local_modes * nfield * rows, width),
            jnp.stack([above[:, :, 0], below[:, :, 0]], axis=1)
            .transpose(2, 1, 0, 3)
            .reshape(2 * nfield * local_modes, width),
        ],
        axis=0,
    )
    partner = lax.ppermute(pack, "modes", [(i, i ^ 1) for i in range(groups)])
    counter = lax.ppermute(pack, "modes", [(i, i ^ 2) for i in range(groups)])
    diagonal = lax.ppermute(counter, "modes", [(i, i ^ 1) for i in range(groups)])
    me = lax.axis_index("modes")
    first_mode = me * local_modes
    weights = lax.dynamic_slice_in_dim(coupling, first_mode, local_modes, 1)
    weights = jnp.concatenate(
        [
            lax.dynamic_slice_in_dim(weights, (me ^ flip) * local_modes, local_modes, 2)
            for flip in range(groups)
        ],
        axis=2,
    )
    weights = jnp.pad(weights, ((0, 0), (0, PAD_I - local_modes), (0, 0)))
    vmem = pl.BlockSpec(memory_space=pltpu.VMEM)
    smem = pl.BlockSpec(memory_space=pltpu.SMEM)
    tables = (kl_field, material, char_state, material_table, char_table, expansion_table)
    comps = nfield + 2
    params = pltpu.CompilerParams(vmem_limit_bytes=48 * 1024 * 1024)
    nmat, nchar = material_table.shape[1], char_table.shape[1]

    def padded(count):
        return -(-count * local_modes // 16) * 16

    def columns(groups_of_blocks):
        pieces = []
        for lo, hi in groups_of_blocks:
            pieces.append(weights[:, :, lo * local_modes:hi * local_modes])
            gap = padded(hi - lo) - (hi - lo) * local_modes
            if gap:
                pieces.append(jnp.zeros((terms, PAD_I, gap), weights.dtype))
        cat = jnp.concatenate(pieces, axis=2)
        return cat.reshape(terms * PAD_I, cat.shape[2])

    def scratch(count):
        return [
            pltpu.VMEM((padded(count) * JS, width), jnp.float32),
            pltpu.VMEM((2 * local_modes * nfield, width), jnp.float32),
        ]

    mix_scratch = [pltpu.VMEM((PAD_I * OS, width), jnp.float32)]
    coef = jax.ShapeDtypeStruct((terms, rows, width), jnp.float32)

    def mix_cost(span):
        return pl.CostEstimate(
            flops=2 * terms * PAD_I * span * comps * rows * width, transcendentals=0,
            bytes_accessed=span * comps * rows * width * 2 + fields.size * 8,
        )

    partial, cond, expand = pl.pallas_call(
        functools.partial(kernel, 2, False, True, False, True, nfield, rows, width, terms, nmat, nchar),
        out_shape=(jax.ShapeDtypeStruct(fields.shape, jnp.float32), coef, coef),
        in_specs=[vmem] * 6 + [smem] * 3,
        out_specs=(vmem, vmem, vmem),
        scratch_shapes=scratch(2) + mix_scratch,
        compiler_params=params,
        cost_estimate=mix_cost(padded(2)),
    )(pack, partner, columns([(0, 2)]), *tables)
    ops = pl.pallas_call(
        functools.partial(kernel, 1, False, False, False, False, nfield, rows, width, terms, nmat, nchar),
        out_shape=jax.ShapeDtypeStruct((rows, padded(1), comps * width), jnp.bfloat16),
        in_specs=[vmem],
        out_specs=vmem,
        scratch_shapes=scratch(1),
        compiler_params=params,
        cost_estimate=pl.CostEstimate(
            flops=12 * padded(1) * comps * rows * width, transcendentals=0,
            bytes_accessed=pack.size * 2 + rows * padded(1) * comps * width * 2,
        ),
    )(counter)
    return pl.pallas_call(
        functools.partial(kernel, 1, True, True, True, False, nfield, rows, width, terms, nmat, nchar),
        out_shape=jax.ShapeDtypeStruct(fields.shape, fields.dtype),
        in_specs=[vmem] * 6,
        out_specs=vmem,
        scratch_shapes=scratch(1) + mix_scratch,
        compiler_params=params,
        cost_estimate=mix_cost(2 * padded(1)),
    )(diagonal, ops, columns([(2, 3), (3, 4)]), cond, expand, partial)


def solution(mesh):
    return jax.shard_map(
        body,
        mesh=mesh,
        in_specs=(
            P("modes", None, "cells", None),
            P(),
            P(None, "cells", None),
            P("cells", None),
            P("cells", None),
            P(),
            P(),
            P(),
        ),
        out_specs=P("modes", None, "cells", None),
        check_vma=False,
    )
```

```python
import functools

import jax
import jax.numpy as jnp
from jax import lax
from jax.experimental import pallas as pl
from jax.experimental.pallas import tpu as pltpu
from jax.sharding import PartitionSpec as P


PAD_I = 24
JS = 73
OS = 65


def edge_rows(cells, axis, dim):
    count = lax.axis_size(axis)
    ends = count - 1
    head = lax.slice_in_dim(cells, 0, 1, axis=dim)
    tail = lax.slice_in_dim(cells, cells.shape[dim] - 1, cells.shape[dim], axis=dim)
    above = lax.ppermute(tail, axis, [(i, (i + 1) % count) for i in range(ends)])
    below = lax.ppermute(head, axis, [((i + 1) % count, i) for i in range(ends)])
    return above, below


def kernel(nblock, prev, final, partial, make, nfield, rows, width, terms, nmat, nchar, *refs):
    blocks = refs[:nblock]
    refs = refs[nblock:]
    if prev:
        prev_ref, refs = refs[0], refs[1:]
    if final and make:
        cp_ref, kl_ref, mat_ref, chr_ref, mt_ref, ct_ref, et_ref = refs[:7]
        refs = refs[7:]
        if partial:
            part_ref, refs = refs[0], refs[1:]
        out_ref, cs, es, fs, hs, os = refs
    elif final:
        cp_ref, cs, es = refs[:3]
        refs = refs[3:]
        if partial:
            part_ref, refs = refs[0], refs[1:]
        out_ref, fs, hs, os = refs
    else:
        out_ref, fs, hs = refs
    nloc = blocks[0].shape[0] // (nfield * (rows + 2))
    nmode = nblock * nloc
    span = fs.shape[0] // JS
    core = nfield * rows
    per = nloc * nfield

    if final and make:
        mat = mat_ref[...]
        chs = chr_ref[...]
        for k in range(terms):
            mv = jnp.zeros((rows, width), jnp.float32)
            ev = jnp.zeros((rows, width), jnp.float32)
            for m in range(nmat):
                hit = mat == m
                mv = jnp.where(hit, mt_ref[k, m], mv)
                ev = jnp.where(hit, et_ref[k, m], ev)
            cv = jnp.zeros((rows, width), jnp.float32)
            for q in range(nchar):
                cv = jnp.where(chs == q, ct_ref[k, q], cv)
            kl = kl_ref[k]
            cs[k] = kl * mv * cv
            es[k] = kl * ev

    for d, blk in enumerate(blocks):
        for jl in range(nloc):
            j = d * nloc + jl
            fs[pl.ds(j * JS, core), :] = blk[pl.ds(jl * core, core), :].astype(jnp.float32)
        hs[...] = blk[pl.ds(nloc * core, 2 * per), :].astype(jnp.float32)
        for side in range(2 * nfield):
            fs[pl.ds(d * nloc * JS + core + side, nloc, stride=JS), :] = hs[pl.ds(side * nloc, nloc), :]
    if span > nmode:
        fs[pl.ds(nmode * JS, (span - nmode) * JS), :] = jnp.zeros(((span - nmode) * JS, width), jnp.float32)

    lane = lax.broadcasted_iota(jnp.int32, (span, width), 1)
    first = lane == 0
    last = lane == width - 1

    def row(r):
        return fs[pl.ds(r, span, stride=JS), :]

    def derive(x):
        comps = []
        grads = None
        for f in range(nfield):
            up = jnp.where(x == 0, core + 2 * f, f * rows + x - 1)
            down = jnp.where(x == rows - 1, core + 2 * f + 1, f * rows + x + 1)
            center = row(f * rows + x)
            above = row(up)
            below = row(down)
            left = jnp.where(first, 0.0, pltpu.roll(center, 1, 1))
            right = jnp.where(last, 0.0, pltpu.roll(center, width - 1, 1))
            lap = 4.0 * center - above - below - left - right
            comps.append(lap.astype(jnp.bfloat16))
            if f == 0:
                gx = 0.5 * (below - above)
                gy = 0.5 * (right - left)
                grads = (gx.astype(jnp.bfloat16), gy.astype(jnp.bfloat16))
        return jnp.concatenate(comps + list(grads), axis=1)

    if not final:
        def keep(x, carry):
            out_ref[x] = derive(x)
            return carry

        lax.fori_loop(0, rows, keep, 0, unroll=8)
        return

    def step(x, carry):
        operand = derive(x)
        if prev:
            operand = jnp.concatenate([prev_ref[x], operand], axis=0)
        mixed = jnp.dot(cp_ref[...], operand, preferred_element_type=jnp.float32)
        cvals = [jnp.broadcast_to(cs[k, pl.ds(x, 1), :], (PAD_I, width)) for k in range(terms)]
        evals = [jnp.broadcast_to(es[k, pl.ds(x, 1), :], (PAD_I, width)) for k in range(terms)]
        for f in range(nfield):
            diffuse = None
            for k in range(terms):
                part = cvals[k] * mixed[k * PAD_I:(k + 1) * PAD_I, f * width:(f + 1) * width]
                diffuse = part if diffuse is None else diffuse + part
            if f in (1, 2):
                c = nfield + f - 1
                strain = None
                for k in range(terms):
                    part = evals[k] * mixed[k * PAD_I:(k + 1) * PAD_I, c * width:(c + 1) * width]
                    strain = part if strain is None else strain + part
                diffuse = diffuse - strain
            os[pl.ds(f * rows + x, PAD_I, stride=OS), :] = diffuse
        return carry

    lax.fori_loop(0, rows, step, 0, unroll=16)

    for i in range(out_ref.shape[0]):
        value = os[pl.ds(i * OS, core), :].reshape(nfield, rows, width)
        if partial:
            value = value + part_ref[i]
        out_ref[i] = value.astype(out_ref.dtype)


def body(
    fields, coupling, kl_field, material, char_state, material_table, char_table, expansion_table
):
    local_modes, nfield, rows, width = fields.shape
    terms = coupling.shape[0]
    groups = lax.axis_size("modes")
    assert groups == 4
    above, below = edge_rows(fields, "cells", 2)
    pack = jnp.concatenate(
        [
            fields.reshape(local_modes * nfield * rows, width),
            jnp.stack([above[:, :, 0], below[:, :, 0]], axis=1)
            .transpose(2, 1, 0, 3)
            .reshape(2 * nfield * local_modes, width),
        ],
        axis=0,
    )
    partner = lax.ppermute(pack, "modes", [(i, i ^ 1) for i in range(groups)])
    counter = lax.ppermute(pack, "modes", [(i, i ^ 2) for i in range(groups)])
    diagonal = lax.ppermute(counter, "modes", [(i, i ^ 1) for i in range(groups)])
    me = lax.axis_index("modes")
    first_mode = me * local_modes
    weights = lax.dynamic_slice_in_dim(coupling, first_mode, local_modes, 1)
    weights = jnp.concatenate(
        [
            lax.dynamic_slice_in_dim(weights, (me ^ flip) * local_modes, local_modes, 2)
            for flip in range(groups)
        ],
        axis=2,
    )
    weights = jnp.pad(weights, ((0, 0), (0, PAD_I - local_modes), (0, 0)))
    vmem = pl.BlockSpec(memory_space=pltpu.VMEM)
    smem = pl.BlockSpec(memory_space=pltpu.SMEM)
    tables = (kl_field, material, char_state, material_table, char_table, expansion_table)
    comps = nfield + 2
    params = pltpu.CompilerParams(vmem_limit_bytes=48 * 1024 * 1024)
    nmat, nchar = material_table.shape[1], char_table.shape[1]

    def padded(count, unit=16):
        return -(-count * local_modes // unit) * unit

    def columns(groups_of_blocks):
        pieces = []
        for n, (lo, hi) in enumerate(groups_of_blocks):
            pieces.append(weights[:, :, lo * local_modes:hi * local_modes])
            unit = 8 if n == len(groups_of_blocks) - 1 and len(groups_of_blocks) > 1 else 16
            gap = padded(hi - lo, unit) - (hi - lo) * local_modes
            if gap:
                pieces.append(jnp.zeros((terms, PAD_I, gap), weights.dtype))
        cat = jnp.concatenate(pieces, axis=2)
        return cat.reshape(terms * PAD_I, cat.shape[2])

    def scratch(count, unit=16):
        return [
            pltpu.VMEM((padded(count, unit) * JS, width), jnp.float32),
            pltpu.VMEM((2 * local_modes * nfield, width), jnp.float32),
        ]

    mix_scratch = [pltpu.VMEM((PAD_I * OS, width), jnp.float32)]
    coef = jax.ShapeDtypeStruct((terms, rows, width), jnp.float32)

    def mix_cost(span):
        return pl.CostEstimate(
            flops=2 * terms * PAD_I * span * comps * rows * width, transcendentals=0,
            bytes_accessed=span * comps * rows * width * 2 + fields.size * 8,
        )

    partial, cond, expand = pl.pallas_call(
        functools.partial(kernel, 2, False, True, False, True, nfield, rows, width, terms, nmat, nchar),
        out_shape=(jax.ShapeDtypeStruct(fields.shape, jnp.float32), coef, coef),
        in_specs=[vmem] * 6 + [smem] * 3,
        out_specs=(vmem, vmem, vmem),
        scratch_shapes=scratch(2) + mix_scratch,
        compiler_params=params,
        cost_estimate=mix_cost(padded(2)),
    )(pack, partner, columns([(0, 2)]), *tables)
    ops = pl.pallas_call(
        functools.partial(kernel, 1, False, False, False, False, nfield, rows, width, terms, nmat, nchar),
        out_shape=jax.ShapeDtypeStruct((rows, padded(1), comps * width), jnp.bfloat16),
        in_specs=[vmem],
        out_specs=vmem,
        scratch_shapes=scratch(1),
        compiler_params=params,
        cost_estimate=pl.CostEstimate(
            flops=12 * padded(1) * comps * rows * width, transcendentals=0,
            bytes_accessed=pack.size * 2 + rows * padded(1) * comps * width * 2,
        ),
    )(counter)
    return pl.pallas_call(
        functools.partial(kernel, 1, True, True, True, False, nfield, rows, width, terms, nmat, nchar),
        out_shape=jax.ShapeDtypeStruct(fields.shape, fields.dtype),
        in_specs=[vmem] * 6,
        out_specs=vmem,
        scratch_shapes=scratch(1, 8) + mix_scratch,
        compiler_params=params,
        cost_estimate=mix_cost(padded(1) + padded(1, 8)),
    )(diagonal, ops, columns([(2, 3), (3, 4)]), cond, expand, partial)


def solution(mesh):
    return jax.shard_map(
        body,
        mesh=mesh,
        in_specs=(
            P("modes", None, "cells", None),
            P(),
            P(None, "cells", None),
            P("cells", None),
            P("cells", None),
            P(),
            P(),
            P(),
        ),
        out_specs=P("modes", None, "cells", None),
        check_vma=False,
    )
```
